32 devices in a mesh: section: 2 (over y), dp: 2 (over x), expert: 8 (over z, core).
Axes of the slice: x: 2, y: 2, z: 4, core: 2. Of those that a mesh axis runs over, the one named last changes fastest.
Arguments:
- activations: bfloat16 [2, 2048, 4096], P('section', ('dp', 'expert')), may hold values from -6 to 6
- norm_gain: float32 [2, 4096], P('section'), may hold values from 0.25 to 1.75
- route_ids: int32 [2, 2048, 2], P('section', ('dp', 'expert')), may hold values from 0 to 3, all different within a row; in each aligned block of 128 rows (0 to 127, 128 to 255, ..., all dimensions but the last counted through in order) at most 72 rows name the same one
- route_gates: float32 [2, 2048, 2], P('section', ('dp', 'expert')), may hold values from 0.2 to 1
- gate_weight: bfloat16 [2, 4096, 3072], P('section', None, 'expert'), may hold values from -0.09375 to 0.09375
- up_weight: bfloat16 [2, 4096, 3072], P('section', None, 'expert'), may hold values from -0.09375 to 0.09375
- leak_rates: float32 [2, 3072], P('section', 'expert'), may hold values from 0.2 to 0.9
- down_weight: bfloat16 [2, 3072, 4096], P('section', 'expert', 'dp'), may hold values from -0.21875 to 0.21875
- cotangent: bfloat16 [2, 2048, 4096], P('section', ('dp', 'expert')), may hold values from -6 to 6
Outputs:
- passed_on: bfloat16 [2, 2048, 4096], P('section', ('dp', 'expert'))
- passed_back: bfloat16 [2, 2048, 4096], P('section', ('dp', 'expert'))
- up_grad: bfloat16 [2, 4096, 3072], P('section', 'dp', 'expert')
The draws below stay inside these ranges and needn't reach their ends.
Inputs may be any that keep to these rules, and one draw needn't show every extreme that they name: `route_ids`: within one section, the 128 tokens of one device name each expert at most 72 times, and some device reaches 72 for some expert; the two experts of a token differ.
All inputs are finite; a program needn't handle non-finite values.
Results may differ from the reference program's by a relative error of at most 0.015.
Values may be sent and summed in bfloat16 or wider, within the bound.
No kernel may reach another device: no remote copies, remote signals or barrier semaphores. Data moves between devices by JAX's collectives and lax.ppermute only.
A program may use at most 192 MiB of HBM per device.

```python
import math
import jax
import jax.numpy as jnp
import numpy as np
from jax import lax

D = 4096
FFW = 768
TSTEPS = 4
TOK_DEV = 128
EXPERTS = 4
CAP = 72
TOKENS = 2048
N_SECTION = 2
N_DP = 2
N_EXPERT = 8


def levels(own_key, dims, cuts, low, top_value):
    gain, own = 1.0, jax.random.fold_in(own_key, 6)
    for axis_at, blocks in cuts:
        steps = jnp.exp(jax.random.uniform(jax.random.fold_in(own, axis_at), (blocks,), jnp.float32, low / len(cuts), top_value / len(cuts)))
        gain = gain * jnp.repeat(steps, dims[axis_at] // blocks).reshape([-1 if axis == axis_at else 1 for axis in range(len(dims))])
    return gain


def shared_out(stream_key, own, number, rows, number_of, top, bound, slope):
    sequence = jax.random.permutation(stream_key, number_of)
    heavy_load, common = shares(number_of, rows * top, bound, slope, True), shares(number_of, rows * top, bound, slope, False)
    places = jnp.arange(number_of)

    def named(tallies, offset_by):
        used = int((tallies > 0).sum())
        fixed = max(1, used // 4)
        moved = fixed + (places - fixed + offset_by * (used - fixed)) % max(1, number_of - fixed)
        return jnp.zeros((number_of,), jnp.int32).at[sequence[jnp.where(places < fixed, places, moved)]].set(jnp.asarray(tallies, jnp.int32))

    tallies = jnp.where(number % 4 == 0, named(heavy_load, number // 4), named(common, number - number // 4 - 1))
    mixed = jax.random.permutation(jax.random.fold_in(own, 3), number_of)
    source_of, receiver = mixed[0:number_of // 2 * 2:2], mixed[1:number_of // 2 * 2:2]
    slack = jnp.minimum(tallies[source_of] - 1, bound - tallies[receiver]) // 2
    slack = jnp.where((source_of == sequence[0]) | (receiver == sequence[0]) | (tallies[receiver] == 0), 0, jnp.maximum(slack, 0))
    moved = jax.random.randint(jax.random.fold_in(own, 4), (number_of // 2,), 0, 1 << 20) % (slack + 1)
    tallies = tallies.at[source_of].add(-moved).at[receiver].add(moved)
    members = jnp.searchsorted(jnp.cumsum(tallies), jnp.arange(rows * top), side="right").astype(jnp.int32)
    grid = members.reshape(top, rows).T
    grid = grid[jax.random.permutation(jax.random.fold_in(own, 1), rows)]
    offset_by = jax.random.randint(jax.random.fold_in(own, 2), (rows, 1), 0, top)
    return jnp.take_along_axis(grid, (jnp.arange(top)[None, :] + offset_by) % top, axis=1)


def shares(amount, total, bound, lean, full):
    weights = [(1 << 20) // math.isqrt(grade ** lean) + 1 for grade in range(1, amount + 1)]
    largest = bound if full else min(bound, max(-(-total // amount), total * weights[0] // sum(weights)))
    least = 1 if total - largest >= amount - 1 else 0
    holding, surplus = [largest] + [least] * (amount - 1), total - largest - least * (amount - 1)
    while surplus > 0:
        movable = [i for i in range(1, amount) if holding[i] < largest] or [i for i in range(1, amount) if holding[i] < bound]
        pool, remaining = sum([weights[i] for i in movable]), surplus
        for i in movable:
            addition = min(bound - holding[i], max(1, remaining * weights[i] // pool), surplus)
            holding[i] = holding[i] + addition
            surplus = surplus - addition
    return np.array(holding)


def normal_values(stream_key, shape, scale, limit, pieces=(), kind=jnp.bfloat16):
    drawn = jax.random.normal(stream_key, shape, jnp.float32) * scale
    if len(pieces) > 0:
        drawn = levels(stream_key, shape, pieces, -0.22, 0.18) * drawn
    return jnp.clip(drawn, min=-limit, max=limit).astype(kind)


def setup_inputs(seed: int = 0) -> dict:
    arg_keys = jax.random.split(jax.random.key(seed), 10)
    activations = normal_values(arg_keys[0], (N_SECTION, TOKENS, D), 1.0, 6.0, ((0, 2), (1, 16)))
    norm_gain = jnp.clip(1.0 + 0.15 * jax.random.normal(arg_keys[1], (N_SECTION, D), jnp.float32), 0.25, 1.75)
    route_ids_keys = jax.random.split(jax.random.fold_in(arg_keys[2], 1), N_SECTION * TOKENS // TOK_DEV)
    route_ids_turns = jax.random.permutation(jax.random.fold_in(arg_keys[2], 3), N_SECTION * TOKENS // TOK_DEV)
    route_ids = jax.vmap(lambda own, number: shared_out(jax.random.fold_in(arg_keys[2], 2), own, number, TOK_DEV, EXPERTS, 2, CAP, 2))(route_ids_keys, route_ids_turns).reshape((N_SECTION, TOKENS, 2))
    route_gates = jnp.clip(0.2 + 0.8 * jax.random.uniform(arg_keys[3], (N_SECTION, TOKENS, 2), jnp.float32) ** levels(arg_keys[3], (N_SECTION, TOKENS, 2), ((0, 2), (1, 16)), -0.2, 0.2), 0.2, 1.0)
    gate_weight = normal_values(arg_keys[4], (N_SECTION, D, EXPERTS * FFW), D ** -0.5, 0.09375, ((0, 2), (2, 8)))
    up_weight = normal_values(arg_keys[5], (N_SECTION, D, EXPERTS * FFW), D ** -0.5, 0.09375, ((0, 2), (2, 8)))
    leak_rates = jnp.clip(jnp.exp(math.log(0.9) - 1.50407736 * jax.random.uniform(arg_keys[6], (N_SECTION, EXPERTS * FFW), jnp.float32) ** levels(arg_keys[6], (N_SECTION, EXPERTS * FFW), ((0, 2), (1, 8)), -0.2, 0.2)), 0.2, 0.9)
    down_weight = normal_values(arg_keys[7], (N_SECTION, EXPERTS * FFW, D), FFW ** -0.5, 0.21875, ((0, 2), (1, 8), (2, 2)))
    cotangent = normal_values(arg_keys[8], (N_SECTION, TOKENS, D), 1.0, 6.0, ((0, 2), (1, 16)))
    return dict(activations=activations, norm_gain=norm_gain, route_ids=route_ids, route_gates=route_gates, gate_weight=gate_weight, up_weight=up_weight, leak_rates=leak_rates, down_weight=down_weight, cotangent=cotangent)


EPS = 1e-06
THETA = 0.5
SHARP = 4.0

def lif_rate(gate_act, up_act, leak_rate):
    drive = jax.nn.silu(gate_act) * up_act
    volts = jnp.zeros_like(drive)
    spike_sum = jnp.zeros_like(drive)
    for timestep in range(TSTEPS):
        volts = leak_rate * volts + drive
        spikes = jax.nn.sigmoid(SHARP * (volts - THETA)) - jax.nn.sigmoid(SHARP * (-volts - THETA))
        volts = volts - THETA * spikes
        spike_sum = spike_sum + spikes
    return spike_sum / TSTEPS

def section_pass(tokens_in, gain_row, ids_section, gates_section, gate_section, up_section, leak_section, down_section, grad_section):
    device_count = N_DP * N_EXPERT
    token_count = tokens_in.shape[0]
    tokens = tokens_in.astype(jnp.float32)
    inv_rms = lax.rsqrt(lax.optimization_barrier(jnp.mean(tokens * tokens, axis=-1, keepdims=True)) + EPS)
    normed = (tokens * inv_rms * gain_row).astype(jnp.bfloat16)
    flat_ids = ids_section.reshape(device_count, TOK_DEV * 2)
    onehot = (flat_ids[:, :, None] == jnp.arange(EXPERTS, dtype=jnp.int32)[None, None, :]).astype(jnp.int32)
    slot_index = lax.optimization_barrier(jnp.sum(onehot * (jnp.cumsum(onehot, axis=1) - 1), axis=2))
    places = jnp.arange(device_count, dtype=jnp.int32)[:, None] * CAP + slot_index
    sentinel = token_count * 2
    slot_table = jnp.full((EXPERTS, device_count * CAP), sentinel, jnp.int32)
    slot_table = slot_table.at[flat_ids.reshape(-1), places.reshape(-1)].set(jnp.arange(token_count * 2, dtype=jnp.int32))
    normed_pad = jnp.concatenate([normed, jnp.zeros((1, D), jnp.bfloat16)], axis=0)
    grad_pad = jnp.concatenate([grad_section.astype(jnp.float32), jnp.zeros((1, D), jnp.float32)], axis=0)
    gate_pad = jnp.concatenate([gates_section.reshape(-1).astype(jnp.float32), jnp.zeros((1,), jnp.float32)], axis=0)

    def per_expert(carry, expert):
        moe_sum, input_grad = carry
        route_rows = slot_table[expert]
        token_rows = route_rows // 2
        route_gate = gate_pad[route_rows]
        inputs = normed_pad[token_rows]
        column = (expert * FFW).astype(jnp.int32)
        gate_part = lax.dynamic_slice_in_dim(gate_section, column, FFW, 1)
        up_part = lax.dynamic_slice_in_dim(up_section, column, FFW, 1)
        leak_part = lax.dynamic_slice_in_dim(leak_section, column, FFW, 0)
        down_part = lax.dynamic_slice_in_dim(down_section, column, FFW, 0)
        gate_act = jnp.dot(inputs, gate_part, preferred_element_type=jnp.float32)
        up_act = jnp.dot(inputs, up_part, preferred_element_type=jnp.float32)
        spike_rate = lif_rate(gate_act, up_act, leak_part).astype(jnp.bfloat16)
        expert_out = jnp.dot(spike_rate, down_part, preferred_element_type=jnp.float32).astype(jnp.bfloat16).astype(jnp.float32)
        moe_sum = moe_sum.at[token_rows].add(route_gate[:, None] * expert_out)
        route_grad = (route_gate[:, None] * grad_pad[token_rows]).astype(jnp.bfloat16)
        rate_grad = lax.dot_general(route_grad, down_part, (((1,), (1,)), ((), ())), preferred_element_type=jnp.float32)
        unused_rate, pullback = jax.vjp(lambda gate_in, up_in: lif_rate(gate_in, up_in, leak_part), gate_act, up_act)
        gate_grad, up_act_grad = pullback(rate_grad)
        gate_grad = gate_grad.astype(jnp.bfloat16)
        up_act_grad = up_act_grad.astype(jnp.bfloat16)
        first = lax.dot_general(gate_grad, gate_part, (((1,), (1,)), ((), ())), preferred_element_type=jnp.float32)
        second = lax.dot_general(up_act_grad, up_part, (((1,), (1,)), ((), ())), preferred_element_type=jnp.float32)
        route_back = (first + second).astype(jnp.bfloat16).astype(jnp.float32)
        input_grad = input_grad.at[token_rows].add(route_back)
        grouped = jnp.einsum('grd,grf->gdf', inputs.reshape(N_DP, N_EXPERT * CAP, D).astype(jnp.float32), up_act_grad.reshape(N_DP, N_EXPERT * CAP, FFW).astype(jnp.float32), precision=lax.Precision.HIGHEST)
        expert_grad = lax.optimization_barrier(jnp.sum(grouped.astype(jnp.bfloat16).astype(jnp.float32), axis=0)).astype(jnp.bfloat16)
        return ((moe_sum, input_grad), expert_grad)
    start = (jnp.zeros((token_count + 1, D), jnp.float32), jnp.zeros((token_count + 1, D), jnp.float32))
    (moe_sum, input_grad), expert_grads = lax.scan(per_expert, start, jnp.arange(EXPERTS, dtype=jnp.int32))
    section_out = (tokens + moe_sum[:token_count]).astype(jnp.bfloat16)
    norm_grad = input_grad[:token_count] * gain_row
    section_back = grad_section.astype(jnp.float32) + inv_rms * norm_grad - tokens * (inv_rms * inv_rms * inv_rms) * lax.optimization_barrier(jnp.mean(tokens * norm_grad, axis=-1, keepdims=True))
    up_grad = jnp.transpose(expert_grads, (1, 0, 2)).reshape(D, EXPERTS * FFW)
    return (section_out, section_back.astype(jnp.bfloat16), up_grad)

def reference(activations, norm_gain, route_ids, route_gates, gate_weight, up_weight, leak_rates, down_weight, cotangent):
    outputs = []
    backs = []
    grads = []
    for section_index in range(N_SECTION):
        section_out, section_back, up_grad = section_pass(activations[section_index], norm_gain[section_index], route_ids[section_index], route_gates[section_index], gate_weight[section_index], up_weight[section_index], leak_rates[section_index], down_weight[section_index], cotangent[section_index])
        outputs.append(section_out)
        backs.append(section_back)
        grads.append(up_grad)
    outputs = jnp.stack(outputs)
    backs = jnp.stack(backs)
    passed_on = jnp.concatenate([jnp.zeros_like(outputs[:1]), outputs[:-1]], axis=0)
    passed_back = jnp.concatenate([backs[1:], jnp.zeros_like(backs[:1])], axis=0)
    return (passed_on, passed_back, jnp.stack(grads))
```

```python
import jax
import jax.numpy as jnp
from jax import lax
from jax.sharding import Mesh, PartitionSpec as P

TSTEPS = 4


EPS = 1e-06
THETA = 0.5
SHARP = 4.0


def passed_along(value, axis, steps):
    count = lax.axis_size(axis)
    leading, last = (max(0, -steps), min(count, count - steps))
    return lax.ppermute(value, axis, [(source, source + steps) for source in range(leading, last)])


def lif_rate(gate_act, up_act, leak_rate):
    drive = jax.nn.silu(gate_act) * up_act
    volts = jnp.zeros_like(drive)
    spike_sum = jnp.zeros_like(drive)
    for timestep in range(TSTEPS):
        volts = leak_rate * volts + drive
        spikes = jax.nn.sigmoid(SHARP * (volts - THETA)) - jax.nn.sigmoid(SHARP * (-volts - THETA))
        volts = volts - THETA * spikes
        spike_sum = spike_sum + spikes
    return spike_sum / TSTEPS


def swap_cores(value):
    return lax.ppermute(value, "core", [(0, 1), (1, 0)])


def to_experts(slot_rows):
    model_width = slot_rows.shape[2]
    mine = lax.all_to_all(slot_rows, "chip", split_axis=0, concat_axis=0, tiled=True)
    both = jnp.concatenate([mine, swap_cores(mine)], axis=0)
    return both.reshape(-1, model_width)


def from_experts(partials, experts, capacity):
    model_width = partials.shape[1]
    paired = partials.reshape(2, experts, capacity, model_width)
    other = swap_cores(paired[1].astype(jnp.bfloat16))
    summed = (paired[0] + other.astype(jnp.float32)).astype(jnp.bfloat16)
    returned = lax.all_to_all(summed, "chip", split_axis=0, concat_axis=0, tiled=True)
    return returned.reshape(experts * capacity, model_width).astype(jnp.float32)


def per_device(
    activations,
    norm_gain,
    route_ids,
    route_gates,
    gate_weight,
    up_weight,
    leak_rates,
    down_weight,
    cotangent,
):
    tok_count = activations.shape[1]
    model_width = activations.shape[2]
    experts = lax.axis_size("chip")
    capacity = min(tok_count, 2 * (9 * tok_count // (8 * experts)))
    tokens = activations[0].astype(jnp.float32)
    gain_row = norm_gain[0]
    inv_rms = lax.rsqrt(jnp.mean(tokens * tokens, axis=-1, keepdims=True) + EPS)
    normed = (tokens * inv_rms * gain_row).astype(jnp.bfloat16)
    flat_ids = route_ids[0].reshape(-1)
    onehot = (flat_ids[:, None] == jnp.arange(experts, dtype=jnp.int32)[None, :]).astype(jnp.int32)
    slot_index = jnp.sum(onehot * (jnp.cumsum(onehot, axis=0) - 1), axis=1)
    places = (flat_ids * capacity + slot_index).reshape(tok_count, 2)
    positions = jnp.arange(experts * capacity, dtype=jnp.int32)[:, None]
    pick_first = positions == places[None, :, 0]
    pick_second = positions == places[None, :, 1]
    pick_both = jnp.logical_or(pick_first, pick_second)
    slot_rows = jnp.dot(
        pick_both.astype(jnp.bfloat16), normed, preferred_element_type=jnp.float32
    ).astype(jnp.bfloat16)
    arrived = to_experts(slot_rows.reshape(experts, capacity, model_width))
    gate_local = gate_weight[0]
    up_local = up_weight[0]
    leak_local = leak_rates[0]
    down_full = lax.all_gather(down_weight[0], "dp", axis=1, tiled=True)
    gate_act = jnp.dot(arrived, gate_local, preferred_element_type=jnp.float32)
    up_act = jnp.dot(arrived, up_local, preferred_element_type=jnp.float32)
    spike_rate = lif_rate(gate_act, up_act, leak_local).astype(jnp.bfloat16)
    out_part = jnp.dot(spike_rate, down_full, preferred_element_type=jnp.float32)
    expert_out = from_experts(out_part, experts, capacity)
    weights = route_gates[0]
    mixing = jnp.where(pick_first.T, weights[:, 0:1], 0.0) + jnp.where(
        pick_second.T, weights[:, 1:2], 0.0
    )
    moe_sum = jnp.dot(
        mixing, expert_out, precision=lax.Precision.HIGHEST, preferred_element_type=jnp.float32
    )
    section_out = (tokens + moe_sum).astype(jnp.bfloat16)
    passed_on = passed_along(section_out[None], "section", 1)
    upstream = cotangent[0].astype(jnp.float32)
    grad_first = (weights[:, 0:1] * upstream).astype(jnp.bfloat16)
    grad_second = (weights[:, 1:2] * upstream).astype(jnp.bfloat16)
    grad_slots = jnp.dot(
        pick_first.astype(jnp.bfloat16), grad_first, preferred_element_type=jnp.float32
    )
    grad_slots = grad_slots + jnp.dot(
        pick_second.astype(jnp.bfloat16), grad_second, preferred_element_type=jnp.float32
    )
    grad_rows = to_experts(grad_slots.astype(jnp.bfloat16).reshape(experts, capacity, model_width))
    rate_grad = lax.dot_general(
        grad_rows, down_full, (((1,), (1,)), ((), ())), preferred_element_type=jnp.float32
    )
    unused_rate, pullback = jax.vjp(
        lambda gate_in, up_in: lif_rate(gate_in, up_in, leak_local), gate_act, up_act
    )
    gate_grad, up_act_grad = pullback(rate_grad)
    gate_grad = gate_grad.astype(jnp.bfloat16)
    up_act_grad = up_act_grad.astype(jnp.bfloat16)
    back_part = lax.dot_general(
        gate_grad, gate_local, (((1,), (1,)), ((), ())), preferred_element_type=jnp.float32
    )
    back_part = back_part + lax.dot_general(
        up_act_grad, up_local, (((1,), (1,)), ((), ())), preferred_element_type=jnp.float32
    )
    route_back = from_experts(back_part, experts, capacity)
    norm_grad = (
        jnp.dot(
            pick_both.T.astype(jnp.float32),
            route_back,
            precision=lax.Precision.HIGHEST,
            preferred_element_type=jnp.float32,
        )
        * gain_row
    )
    section_back = (
        upstream
        + inv_rms * norm_grad
        - tokens
        * (inv_rms * inv_rms * inv_rms)
        * jnp.mean(tokens * norm_grad, axis=-1, keepdims=True)
    )
    passed_back = passed_along(section_back.astype(jnp.bfloat16)[None], "section", -1)
    up_term = lax.dot_general(
        arrived, up_act_grad, (((0,), (0,)), ((), ())), preferred_element_type=jnp.float32
    )
    up_term = up_term.astype(jnp.bfloat16).astype(jnp.float32)
    up_grad = lax.psum_scatter(up_term.astype(jnp.bfloat16), "dp", scatter_dimension=0, tiled=True)[
        None
    ]
    return (passed_on, passed_back, up_grad)


def chip_mesh(mesh):
    sections, replicas, width = mesh.devices.shape
    return Mesh(mesh.devices.reshape(sections, replicas, width // 2, 2), ("section", "dp", "chip", "core"))


def solution(mesh):
    tokens = P("section", ("dp", "chip", "core"), None)
    return jax.shard_map(
        per_device,
        mesh=chip_mesh(mesh),
        in_specs=(
            tokens,
            P("section", None),
            tokens,
            tokens,
            P("section", None, ("chip", "core")),
            P("section", None, ("chip", "core")),
            P("section", ("chip", "core")),
            P("section", ("chip", "core"), "dp"),
            tokens,
        ),
        out_specs=(tokens, tokens, P("section", "dp", ("chip", "core"))),
        check_vma=False,
    )
```

```python
import jax
import jax.numpy as jnp
from jax import lax
from jax.sharding import Mesh, PartitionSpec as P

TSTEPS = 4


EPS = 1e-06
THETA = 0.5
SHARP = 4.0


def passed_along(value, axis, steps):
    count = lax.axis_size(axis)
    leading, last = (max(0, -steps), min(count, count - steps))
    return lax.ppermute(value, axis, [(source, source + steps) for source in range(leading, last)])


def lif_rate(gate_act, up_act, leak_rate):
    drive = jax.nn.silu(gate_act) * up_act
    volts = jnp.zeros_like(drive)
    spike_sum = jnp.zeros_like(drive)
    for timestep in range(TSTEPS):
        volts = leak_rate * volts + drive
        spikes = jax.nn.sigmoid(SHARP * (volts - THETA)) - jax.nn.sigmoid(SHARP * (-volts - THETA))
        volts = volts - THETA * spikes
        spike_sum = spike_sum + spikes
    return spike_sum / TSTEPS


def swap_cores(value):
    return lax.ppermute(value, "core", [(0, 1), (1, 0)])


def shifted(value, steps):
    count = lax.axis_size("chip")
    return lax.ppermute(value, "chip", [(source, (source + steps) % count) for source in range(count)])


def to_experts(blocks):
    model_width = blocks.shape[2]
    mine = jnp.stack([blocks[0]] + [shifted(blocks[k], k) for k in range(1, blocks.shape[0])])
    both = jnp.concatenate([mine, swap_cores(mine)], axis=0)
    return both.reshape(-1, model_width)


def from_experts(partials, experts, capacity):
    model_width = partials.shape[1]
    paired = partials.reshape(2, experts, capacity, model_width)
    other = swap_cores(paired[1].astype(jnp.bfloat16))
    summed = (paired[0] + other.astype(jnp.float32)).astype(jnp.bfloat16)
    returned = jnp.stack([summed[0]] + [shifted(summed[k], -k) for k in range(1, experts)])
    return returned.reshape(experts * capacity, model_width).astype(jnp.float32)


def per_device(
    activations,
    norm_gain,
    route_ids,
    route_gates,
    gate_weight,
    up_weight,
    leak_rates,
    down_weight,
    cotangent,
):
    tok_count = activations.shape[1]
    model_width = activations.shape[2]
    experts = lax.axis_size("chip")
    capacity = min(tok_count, 2 * (9 * tok_count // (8 * experts)))
    tokens = activations[0].astype(jnp.float32)
    gain_row = norm_gain[0]
    inv_rms = lax.rsqrt(jnp.mean(tokens * tokens, axis=-1, keepdims=True) + EPS)
    normed = (tokens * inv_rms * gain_row).astype(jnp.bfloat16)
    flat_ids = (route_ids[0].reshape(-1) - lax.axis_index("chip")) % experts
    onehot = (flat_ids[:, None] == jnp.arange(experts, dtype=jnp.int32)[None, :]).astype(jnp.int32)
    slot_index = jnp.sum(onehot * (jnp.cumsum(onehot, axis=0) - 1), axis=1)
    places = (flat_ids * capacity + slot_index).reshape(tok_count, 2)
    positions = jnp.arange(experts * capacity, dtype=jnp.int32)[:, None]
    pick_first = positions == places[None, :, 0]
    pick_second = positions == places[None, :, 1]
    pick_both = jnp.logical_or(pick_first, pick_second)
    slot_rows = jnp.dot(
        pick_both.astype(jnp.bfloat16), normed, preferred_element_type=jnp.float32
    ).astype(jnp.bfloat16)
    arrived = to_experts(slot_rows.reshape(experts, capacity, model_width))
    gate_local = gate_weight[0]
    up_local = up_weight[0]
    leak_local = leak_rates[0]
    down_full = lax.all_gather(down_weight[0], "dp", axis=1, tiled=True)
    gate_act = jnp.dot(arrived, gate_local, preferred_element_type=jnp.float32)
    up_act = jnp.dot(arrived, up_local, preferred_element_type=jnp.float32)
    spike_rate = lif_rate(gate_act, up_act, leak_local).astype(jnp.bfloat16)
    out_part = jnp.dot(spike_rate, down_full, preferred_element_type=jnp.float32)
    expert_out = from_experts(out_part, experts, capacity)
    weights = route_gates[0]
    mixing = jnp.where(pick_first.T, weights[:, 0:1], 0.0) + jnp.where(
        pick_second.T, weights[:, 1:2], 0.0
    )
    moe_sum = jnp.dot(
        mixing, expert_out, precision=lax.Precision.HIGHEST, preferred_element_type=jnp.float32
    )
    section_out = (tokens + moe_sum).astype(jnp.bfloat16)
    passed_on = passed_along(section_out[None], "section", 1)
    upstream = cotangent[0].astype(jnp.float32)
    grad_first = (weights[:, 0:1] * upstream).astype(jnp.bfloat16)
    grad_second = (weights[:, 1:2] * upstream).astype(jnp.bfloat16)
    grad_slots = jnp.dot(
        pick_first.astype(jnp.bfloat16), grad_first, preferred_element_type=jnp.float32
    )
    grad_slots = grad_slots + jnp.dot(
        pick_second.astype(jnp.bfloat16), grad_second, preferred_element_type=jnp.float32
    )
    grad_slots, unused_arrived = lax.optimization_barrier((grad_slots.astype(jnp.bfloat16), arrived))
    grad_rows = to_experts(grad_slots.reshape(experts, capacity, model_width))
    rate_grad = lax.dot_general(
        grad_rows, down_full, (((1,), (1,)), ((), ())), preferred_element_type=jnp.float32
    )
    unused_rate, pullback = jax.vjp(
        lambda gate_in, up_in: lif_rate(gate_in, up_in, leak_local), gate_act, up_act
    )
    gate_grad, up_act_grad = pullback(rate_grad)
    gate_grad = gate_grad.astype(jnp.bfloat16)
    up_act_grad = up_act_grad.astype(jnp.bfloat16)
    back_part = lax.dot_general(
        gate_grad, gate_local, (((1,), (1,)), ((), ())), preferred_element_type=jnp.float32
    )
    back_part = back_part + lax.dot_general(
        up_act_grad, up_local, (((1,), (1,)), ((), ())), preferred_element_type=jnp.float32
    )
    route_back = from_experts(back_part, experts, capacity)
    norm_grad = (
        jnp.dot(
            pick_both.T.astype(jnp.float32),
            route_back,
            precision=lax.Precision.HIGHEST,
            preferred_element_type=jnp.float32,
        )
        * gain_row
    )
    section_back = (
        upstream
        + inv_rms * norm_grad
        - tokens
        * (inv_rms * inv_rms * inv_rms)
        * jnp.mean(tokens * norm_grad, axis=-1, keepdims=True)
    )
    passed_back = passed_along(section_back.astype(jnp.bfloat16)[None], "section", -1)
    up_term = lax.dot_general(
        arrived, up_act_grad, (((0,), (0,)), ((), ())), preferred_element_type=jnp.float32
    )
    up_term = up_term.astype(jnp.bfloat16).astype(jnp.float32)
    up_grad = lax.psum_scatter(up_term.astype(jnp.bfloat16), "dp", scatter_dimension=0, tiled=True)[
        None
    ]
    return (passed_on, passed_back, up_grad)


def chip_mesh(mesh):
    sections, replicas, width = mesh.devices.shape
    return Mesh(mesh.devices.reshape(sections, replicas, width // 2, 2), ("section", "dp", "chip", "core"))


def solution(mesh):
    tokens = P("section", ("dp", "chip", "core"), None)
    return jax.shard_map(
        per_device,
        mesh=chip_mesh(mesh),
        in_specs=(
            tokens,
            P("section", None),
            tokens,
            tokens,
            P("section", None, ("chip", "core")),
            P("section", None, ("chip", "core")),
            P("section", ("chip", "core")),
            P("section", ("chip", "core"), "dp"),
            tokens,
        ),
        out_specs=(tokens, tokens, P("section", "dp", ("chip", "core"))),
        check_vma=False,
    )
```

```python
import jax
import jax.numpy as jnp
from jax import lax
from jax.sharding import Mesh, PartitionSpec as P

TSTEPS = 4


EPS = 1e-06
THETA = 0.5
SHARP = 4.0


def passed_along(value, axis, steps):
    count = lax.axis_size(axis)
    leading, last = (max(0, -steps), min(count, count - steps))
    return lax.ppermute(value, axis, [(source, source + steps) for source in range(leading, last)])


def lif_rate(gate_act, up_act, leak_rate):
    drive = jax.nn.silu(gate_act) * up_act
    volts = jnp.zeros_like(drive)
    spike_sum = jnp.zeros_like(drive)
    for timestep in range(TSTEPS):
        volts = leak_rate * volts + drive
        spikes = jax.nn.sigmoid(SHARP * (volts - THETA)) - jax.nn.sigmoid(SHARP * (-volts - THETA))
        volts = volts - THETA * spikes
        spike_sum = spike_sum + spikes
    return spike_sum / TSTEPS


def swap_cores(value):
    return lax.ppermute(value, "core", [(0, 1), (1, 0)])


def shifted(value, steps):
    count = lax.axis_size("chip")
    return lax.ppermute(value, "chip", [(source, (source + steps) % count) for source in range(count)])


def to_experts(blocks):
    model_width = blocks.shape[2]
    mine = jnp.stack([blocks[0]] + [shifted(blocks[k], k) for k in range(1, blocks.shape[0])])
    both = jnp.concatenate([mine, swap_cores(mine)], axis=0)
    return both.reshape(-1, model_width)


def combine_cores(partials, experts, capacity):
    model_width = partials.shape[1]
    paired = partials.reshape(2, experts, capacity, model_width)
    other = swap_cores(paired[1].astype(jnp.bfloat16))
    return (paired[0] + other.astype(jnp.float32)).astype(jnp.bfloat16)


def from_experts(summed):
    experts, capacity, model_width = summed.shape
    returned = jnp.stack([summed[0]] + [shifted(summed[k], -k) for k in range(1, experts)])
    return returned.reshape(experts * capacity, model_width).astype(jnp.float32)


def per_device(
    activations,
    norm_gain,
    route_ids,
    route_gates,
    gate_weight,
    up_weight,
    leak_rates,
    down_weight,
    cotangent,
):
    tok_count = activations.shape[1]
    model_width = activations.shape[2]
    experts = lax.axis_size("chip")
    capacity = min(tok_count, 2 * (9 * tok_count // (8 * experts)))
    tokens = activations[0].astype(jnp.float32)
    gain_row = norm_gain[0]
    inv_rms = lax.rsqrt(jnp.mean(tokens * tokens, axis=-1, keepdims=True) + EPS)
    normed = (tokens * inv_rms * gain_row).astype(jnp.bfloat16)
    flat_ids = (route_ids[0].reshape(-1) - lax.axis_index("chip")) % experts
    onehot = (flat_ids[:, None] == jnp.arange(experts, dtype=jnp.int32)[None, :]).astype(jnp.int32)
    slot_index = jnp.sum(onehot * (jnp.cumsum(onehot, axis=0) - 1), axis=1)
    places = (flat_ids * capacity + slot_index).reshape(tok_count, 2)
    positions = jnp.arange(experts * capacity, dtype=jnp.int32)[:, None]
    pick_first = positions == places[None, :, 0]
    pick_second = positions == places[None, :, 1]
    pick_both = jnp.logical_or(pick_first, pick_second)
    slot_rows = jnp.dot(
        pick_both.astype(jnp.bfloat16), normed, preferred_element_type=jnp.float32
    ).astype(jnp.bfloat16)
    arrived = to_experts(slot_rows.reshape(experts, capacity, model_width))
    gate_local = gate_weight[0]
    up_local = up_weight[0]
    leak_local = leak_rates[0]
    down_full = lax.all_gather(down_weight[0], "dp", axis=1, tiled=True)
    gate_act = jnp.dot(arrived, gate_local, preferred_element_type=jnp.float32)
    up_act = jnp.dot(arrived, up_local, preferred_element_type=jnp.float32)
    spike_rate = lif_rate(gate_act, up_act, leak_local).astype(jnp.bfloat16)
    out_part = jnp.dot(spike_rate, down_full, preferred_element_type=jnp.float32)
    out_summed = combine_cores(out_part, experts, capacity)
    weights = route_gates[0]
    upstream = cotangent[0].astype(jnp.float32)
    grad_first = (weights[:, 0:1] * upstream).astype(jnp.bfloat16)
    grad_second = (weights[:, 1:2] * upstream).astype(jnp.bfloat16)
    grad_slots = jnp.dot(
        pick_first.astype(jnp.bfloat16), grad_first, preferred_element_type=jnp.float32
    )
    grad_slots = grad_slots + jnp.dot(
        pick_second.astype(jnp.bfloat16), grad_second, preferred_element_type=jnp.float32
    )
    grad_slots, unused_arrived = lax.optimization_barrier((grad_slots.astype(jnp.bfloat16), arrived))
    grad_rows = to_experts(grad_slots.reshape(experts, capacity, model_width))
    grad_rows, out_summed = lax.optimization_barrier((grad_rows, out_summed))
    expert_out = from_experts(out_summed)
    mixing = jnp.where(pick_first.T, weights[:, 0:1], 0.0) + jnp.where(
        pick_second.T, weights[:, 1:2], 0.0
    )
    moe_sum = jnp.dot(
        mixing, expert_out, precision=lax.Precision.HIGHEST, preferred_element_type=jnp.float32
    )
    section_out = (tokens + moe_sum).astype(jnp.bfloat16)
    passed_on = passed_along(section_out[None], "section", 1)
    rate_grad = lax.dot_general(
        grad_rows, down_full, (((1,), (1,)), ((), ())), preferred_element_type=jnp.float32
    )
    unused_rate, pullback = jax.vjp(
        lambda gate_in, up_in: lif_rate(gate_in, up_in, leak_local), gate_act, up_act
    )
    gate_grad, up_act_grad = pullback(rate_grad)
    gate_grad = gate_grad.astype(jnp.bfloat16)
    up_act_grad = up_act_grad.astype(jnp.bfloat16)
    back_part = lax.dot_general(
        gate_grad, gate_local, (((1,), (1,)), ((), ())), preferred_element_type=jnp.float32
    )
    back_part = back_part + lax.dot_general(
        up_act_grad, up_local, (((1,), (1,)), ((), ())), preferred_element_type=jnp.float32
    )
    route_back = from_experts(combine_cores(back_part, experts, capacity))
    norm_grad = (
        jnp.dot(
            pick_both.T.astype(jnp.float32),
            route_back,
            precision=lax.Precision.HIGHEST,
            preferred_element_type=jnp.float32,
        )
        * gain_row
    )
    section_back = (
        upstream
        + inv_rms * norm_grad
        - tokens
        * (inv_rms * inv_rms * inv_rms)
        * jnp.mean(tokens * norm_grad, axis=-1, keepdims=True)
    )
    passed_back = passed_along(section_back.astype(jnp.bfloat16)[None], "section", -1)
    up_term = lax.dot_general(
        arrived, up_act_grad, (((0,), (0,)), ((), ())), preferred_element_type=jnp.float32
    )
    up_term = up_term.astype(jnp.bfloat16).astype(jnp.float32)
    up_grad = lax.psum_scatter(up_term.astype(jnp.bfloat16), "dp", scatter_dimension=0, tiled=True)[
        None
    ]
    return (passed_on, passed_back, up_grad)


def chip_mesh(mesh):
    sections, replicas, width = mesh.devices.shape
    return Mesh(mesh.devices.reshape(sections, replicas, width // 2, 2), ("section", "dp", "chip", "core"))


def solution(mesh):
    tokens = P("section", ("dp", "chip", "core"), None)
    return jax.shard_map(
        per_device,
        mesh=chip_mesh(mesh),
        in_specs=(
            tokens,
            P("section", None),
            tokens,
            tokens,
            P("section", None, ("chip", "core")),
            P("section", None, ("chip", "core")),
            P("section", ("chip", "core")),
            P("section", ("chip", "core"), "dp"),
            tokens,
        ),
        out_specs=(tokens, tokens, P("section", "dp", ("chip", "core"))),
        check_vma=False,
    )
```

```python
import jax
import jax.numpy as jnp
from jax import lax
from jax.sharding import Mesh, PartitionSpec as P

TSTEPS = 4


EPS = 1e-06
THETA = 0.5
SHARP = 4.0


def passed_along(value, axis, steps):
    count = lax.axis_size(axis)
    leading, last = (max(0, -steps), min(count, count - steps))
    return lax.ppermute(value, axis, [(source, source + steps) for source in range(leading, last)])


def lif_rate(gate_act, up_act, leak_rate):
    drive = jax.nn.silu(gate_act) * up_act
    volts = jnp.zeros_like(drive)
    spike_sum = jnp.zeros_like(drive)
    for timestep in range(TSTEPS):
        volts = leak_rate * volts + drive
        spikes = jax.nn.sigmoid(SHARP * (volts - THETA)) - jax.nn.sigmoid(SHARP * (-volts - THETA))
        volts = volts - THETA * spikes
        spike_sum = spike_sum + spikes
    return spike_sum / TSTEPS


def swap_cores(value):
    return lax.ppermute(value, "core", [(0, 1), (1, 0)])


def shifted(value, steps):
    count = lax.axis_size("chip")
    return lax.ppermute(value, "chip", [(source, (source + steps) % count) for source in range(count)])


def to_experts(blocks):
    model_width = blocks.shape[2]
    mine = jnp.stack([blocks[0]] + [shifted(blocks[k], k) for k in range(1, blocks.shape[0])])
    both = jnp.concatenate([mine, swap_cores(mine)], axis=0)
    return both.reshape(-1, model_width)


def combine_cores(partials, experts, capacity):
    model_width = partials.shape[1]
    paired = partials.reshape(2, experts, capacity, model_width)
    other = swap_cores(paired[1].astype(jnp.bfloat16))
    return (paired[0] + other.astype(jnp.float32)).astype(jnp.bfloat16)


def from_experts(*summed):
    experts, capacity, model_width = summed[0].shape
    paired = jnp.stack(summed, axis=1)
    returned = jnp.stack([paired[0]] + [shifted(paired[k], -k) for k in range(1, experts)], axis=1)
    returned = returned.reshape(len(summed), experts * capacity, model_width).astype(jnp.float32)
    return tuple(returned)


def per_device(
    activations,
    norm_gain,
    route_ids,
    route_gates,
    gate_weight,
    up_weight,
    leak_rates,
    down_weight,
    cotangent,
):
    tok_count = activations.shape[1]
    model_width = activations.shape[2]
    experts = lax.axis_size("chip")
    capacity = min(tok_count, 2 * (9 * tok_count // (8 * experts)))
    tokens = activations[0].astype(jnp.float32)
    gain_row = norm_gain[0]
    inv_rms = lax.rsqrt(jnp.mean(tokens * tokens, axis=-1, keepdims=True) + EPS)
    normed = (tokens * inv_rms * gain_row).astype(jnp.bfloat16)
    flat_ids = (route_ids[0].reshape(-1) - lax.axis_index("chip")) % experts
    onehot = (flat_ids[:, None] == jnp.arange(experts, dtype=jnp.int32)[None, :]).astype(jnp.int32)
    slot_index = jnp.sum(onehot * (jnp.cumsum(onehot, axis=0) - 1), axis=1)
    places = (flat_ids * capacity + slot_index).reshape(tok_count, 2)
    positions = jnp.arange(experts * capacity, dtype=jnp.int32)[:, None]
    pick_first = positions == places[None, :, 0]
    pick_second = positions == places[None, :, 1]
    pick_both = jnp.logical_or(pick_first, pick_second)
    slot_rows = jnp.dot(
        pick_both.astype(jnp.bfloat16), normed, preferred_element_type=jnp.float32
    ).astype(jnp.bfloat16)
    arrived = to_experts(slot_rows.reshape(experts, capacity, model_width))
    gate_local = gate_weight[0]
    up_local = up_weight[0]
    leak_local = leak_rates[0]
    down_full = lax.all_gather(down_weight[0], "dp", axis=1, tiled=True)
    gate_act = jnp.dot(arrived, gate_local, preferred_element_type=jnp.float32)
    up_act = jnp.dot(arrived, up_local, preferred_element_type=jnp.float32)
    spike_rate = lif_rate(gate_act, up_act, leak_local).astype(jnp.bfloat16)
    out_part = jnp.dot(spike_rate, down_full, preferred_element_type=jnp.float32)
    out_summed = combine_cores(out_part, experts, capacity)
    weights = route_gates[0]
    upstream = cotangent[0].astype(jnp.float32)
    grad_first = (weights[:, 0:1] * upstream).astype(jnp.bfloat16)
    grad_second = (weights[:, 1:2] * upstream).astype(jnp.bfloat16)
    grad_slots = jnp.dot(
        pick_first.astype(jnp.bfloat16), grad_first, preferred_element_type=jnp.float32
    )
    grad_slots = grad_slots + jnp.dot(
        pick_second.astype(jnp.bfloat16), grad_second, preferred_element_type=jnp.float32
    )
    grad_slots, unused_arrived = lax.optimization_barrier((grad_slots.astype(jnp.bfloat16), arrived))
    grad_rows = to_experts(grad_slots.reshape(experts, capacity, model_width))
    rate_grad = lax.dot_general(
        grad_rows, down_full, (((1,), (1,)), ((), ())), preferred_element_type=jnp.float32
    )
    unused_rate, pullback = jax.vjp(
        lambda gate_in, up_in: lif_rate(gate_in, up_in, leak_local), gate_act, up_act
    )
    gate_grad, up_act_grad = pullback(rate_grad)
    gate_grad = gate_grad.astype(jnp.bfloat16)
    up_act_grad = up_act_grad.astype(jnp.bfloat16)
    back_part = lax.dot_general(
        gate_grad, gate_local, (((1,), (1,)), ((), ())), preferred_element_type=jnp.float32
    )
    back_part = back_part + lax.dot_general(
        up_act_grad, up_local, (((1,), (1,)), ((), ())), preferred_element_type=jnp.float32
    )
    expert_out, route_back = from_experts(out_summed, combine_cores(back_part, experts, capacity))
    mixing = jnp.where(pick_first.T, weights[:, 0:1], 0.0) + jnp.where(
        pick_second.T, weights[:, 1:2], 0.0
    )
    moe_sum = jnp.dot(
        mixing, expert_out, precision=lax.Precision.HIGHEST, preferred_element_type=jnp.float32
    )
    section_out = (tokens + moe_sum).astype(jnp.bfloat16)
    passed_on = passed_along(section_out[None], "section", 1)
    norm_grad = (
        jnp.dot(
            pick_both.T.astype(jnp.float32),
            route_back,
            precision=lax.Precision.HIGHEST,
            preferred_element_type=jnp.float32,
        )
        * gain_row
    )
    section_back = (
        upstream
        + inv_rms * norm_grad
        - tokens
        * (inv_rms * inv_rms * inv_rms)
        * jnp.mean(tokens * norm_grad, axis=-1, keepdims=True)
    )
    passed_back = passed_along(section_back.astype(jnp.bfloat16)[None], "section", -1)
    up_term = lax.dot_general(
        arrived, up_act_grad, (((0,), (0,)), ((), ())), preferred_element_type=jnp.float32
    )
    up_term = up_term.astype(jnp.bfloat16).astype(jnp.float32)
    up_grad = lax.psum_scatter(up_term.astype(jnp.bfloat16), "dp", scatter_dimension=0, tiled=True)[
        None
    ]
    return (passed_on, passed_back, up_grad)


def chip_mesh(mesh):
    sections, replicas, width = mesh.devices.shape
    return Mesh(mesh.devices.reshape(sections, replicas, width // 2, 2), ("section", "dp", "chip", "core"))


def solution(mesh):
    tokens = P("section", ("dp", "chip", "core"), None)
    return jax.shard_map(
        per_device,
        mesh=chip_mesh(mesh),
        in_specs=(
            tokens,
            P("section", None),
            tokens,
            tokens,
            P("section", None, ("chip", "core")),
            P("section", None, ("chip", "core")),
            P("section", ("chip", "core")),
            P("section", ("chip", "core"), "dp"),
            tokens,
        ),
        out_specs=(tokens, tokens, P("section", "dp", ("chip", "core"))),
        check_vma=False,
    )
```

```python
import jax
import jax.numpy as jnp
from jax import lax
from jax.sharding import Mesh, PartitionSpec as P

TSTEPS = 4


EPS = 1e-06
THETA = 0.5
SHARP = 4.0


def passed_along(value, axis, steps):
    count = lax.axis_size(axis)
    leading, last = (max(0, -steps), min(count, count - steps))
    return lax.ppermute(value, axis, [(source, source + steps) for source in range(leading, last)])


def lif_rate(gate_act, up_act, leak_rate):
    drive = jax.nn.silu(gate_act) * up_act
    volts = jnp.zeros_like(drive)
    spike_sum = jnp.zeros_like(drive)
    for timestep in range(TSTEPS):
        volts = leak_rate * volts + drive
        spikes = jax.nn.sigmoid(SHARP * (volts - THETA)) - jax.nn.sigmoid(SHARP * (-volts - THETA))
        volts = volts - THETA * spikes
        spike_sum = spike_sum + spikes
    return spike_sum / TSTEPS


def swap_cores(value):
    return lax.ppermute(value, "core", [(0, 1), (1, 0)])


def shifted(value, steps):
    count = lax.axis_size("chip")
    return lax.ppermute(value, "chip", [(source, (source + steps) % count) for source in range(count)])


def to_experts(blocks):
    model_width = blocks.shape[2]
    mine = jnp.stack([blocks[0]] + [shifted(blocks[k], k) for k in range(1, blocks.shape[0])])
    both = jnp.concatenate([mine, swap_cores(mine)], axis=0)
    return both.reshape(-1, model_width)


def from_experts(partials, experts, capacity):
    model_width = partials.shape[1]
    paired = partials.reshape(2, experts, capacity, model_width)
    other = swap_cores(paired[1].astype(jnp.bfloat16))
    summed = (paired[0] + other.astype(jnp.float32)).astype(jnp.bfloat16)
    returned = jnp.stack([summed[0]] + [shifted(summed[k], -k) for k in range(1, experts)])
    return returned.reshape(experts * capacity, model_width).astype(jnp.float32)


def per_device(
    activations,
    norm_gain,
    route_ids,
    route_gates,
    gate_weight,
    up_weight,
    leak_rates,
    down_weight,
    cotangent,
):
    tok_count = activations.shape[1]
    model_width = activations.shape[2]
    experts = lax.axis_size("chip")
    capacity = min(tok_count, 2 * (9 * tok_count // (8 * experts)))
    tokens = activations[0].astype(jnp.float32)
    gain_row = norm_gain[0]
    inv_rms = lax.rsqrt(jnp.mean(tokens * tokens, axis=-1, keepdims=True) + EPS)
    normed = (tokens * inv_rms * gain_row).astype(jnp.bfloat16)
    flat_ids = (route_ids[0].reshape(-1) - lax.axis_index("chip")) % experts
    onehot = (flat_ids[:, None] == jnp.arange(experts, dtype=jnp.int32)[None, :]).astype(jnp.int32)
    slot_index = jnp.sum(onehot * (jnp.cumsum(onehot, axis=0) - 1), axis=1)
    places = (flat_ids * capacity + slot_index).reshape(tok_count, 2)
    positions = jnp.arange(experts * capacity, dtype=jnp.int32)[:, None]
    pick_first = positions == places[None, :, 0]
    pick_second = positions == places[None, :, 1]
    pick_both = jnp.logical_or(pick_first, pick_second)
    slot_rows = jnp.dot(
        pick_both.astype(jnp.bfloat16), normed, preferred_element_type=jnp.float32
    ).astype(jnp.bfloat16)
    arrived = to_experts(slot_rows.reshape(experts, capacity, model_width))
    gate_local = gate_weight[0]
    up_local = up_weight[0]
    leak_local = leak_rates[0]
    down_full = lax.all_gather(down_weight[0], "dp", axis=1, tiled=True)
    gate_act = jnp.dot(arrived, gate_local, preferred_element_type=jnp.float32)
    up_act = jnp.dot(arrived, up_local, preferred_element_type=jnp.float32)
    spike_exact, lif_pullback = jax.vjp(
        lambda gate_in, up_in: lif_rate(gate_in, up_in, leak_local), gate_act, up_act
    )
    spike_rate = spike_exact.astype(jnp.bfloat16)
    gate_slope, up_slope = lif_pullback(jnp.ones_like(spike_exact))
    out_part = jnp.dot(spike_rate, down_full, preferred_element_type=jnp.float32)
    expert_out = from_experts(out_part, experts, capacity)
    weights = route_gates[0]
    mixing = jnp.where(pick_first.T, weights[:, 0:1], 0.0) + jnp.where(
        pick_second.T, weights[:, 1:2], 0.0
    )
    moe_sum = jnp.dot(
        mixing, expert_out, precision=lax.Precision.HIGHEST, preferred_element_type=jnp.float32
    )
    section_out = (tokens + moe_sum).astype(jnp.bfloat16)
    passed_on = passed_along(section_out[None], "section", 1)
    upstream = cotangent[0].astype(jnp.float32)
    grad_first = (weights[:, 0:1] * upstream).astype(jnp.bfloat16)
    grad_second = (weights[:, 1:2] * upstream).astype(jnp.bfloat16)
    grad_slots = jnp.dot(
        pick_first.astype(jnp.bfloat16), grad_first, preferred_element_type=jnp.float32
    )
    grad_slots = grad_slots + jnp.dot(
        pick_second.astype(jnp.bfloat16), grad_second, preferred_element_type=jnp.float32
    )
    grad_slots, unused_arrived = lax.optimization_barrier((grad_slots.astype(jnp.bfloat16), arrived))
    grad_rows = to_experts(grad_slots.reshape(experts, capacity, model_width))
    rate_grad = lax.dot_general(
        grad_rows, down_full, (((1,), (1,)), ((), ())), preferred_element_type=jnp.float32
    )
    gate_grad = (rate_grad * gate_slope).astype(jnp.bfloat16)
    up_act_grad = (rate_grad * up_slope).astype(jnp.bfloat16)
    back_part = lax.dot_general(
        gate_grad, gate_local, (((1,), (1,)), ((), ())), preferred_element_type=jnp.float32
    )
    back_part = back_part + lax.dot_general(
        up_act_grad, up_local, (((1,), (1,)), ((), ())), preferred_element_type=jnp.float32
    )
    route_back = from_experts(back_part, experts, capacity)
    norm_grad = (
        jnp.dot(
            pick_both.T.astype(jnp.float32),
            route_back,
            precision=lax.Precision.HIGHEST,
            preferred_element_type=jnp.float32,
        )
        * gain_row
    )
    section_back = (
        upstream
        + inv_rms * norm_grad
        - tokens
        * (inv_rms * inv_rms * inv_rms)
        * jnp.mean(tokens * norm_grad, axis=-1, keepdims=True)
    )
    passed_back = passed_along(section_back.astype(jnp.bfloat16)[None], "section", -1)
    up_term = lax.dot_general(
        arrived, up_act_grad, (((0,), (0,)), ((), ())), preferred_element_type=jnp.float32
    )
    up_term = up_term.astype(jnp.bfloat16).astype(jnp.float32)
    up_grad = lax.psum_scatter(up_term.astype(jnp.bfloat16), "dp", scatter_dimension=0, tiled=True)[
        None
    ]
    return (passed_on, passed_back, up_grad)


def chip_mesh(mesh):
    sections, replicas, width = mesh.devices.shape
    return Mesh(mesh.devices.reshape(sections, replicas, width // 2, 2), ("section", "dp", "chip", "core"))


def solution(mesh):
    tokens = P("section", ("dp", "chip", "core"), None)
    return jax.shard_map(
        per_device,
        mesh=chip_mesh(mesh),
        in_specs=(
            tokens,
            P("section", None),
            tokens,
            tokens,
            P("section", None, ("chip", "core")),
            P("section", None, ("chip", "core")),
            P("section", ("chip", "core")),
            P("section", ("chip", "core"), "dp"),
            tokens,
        ),
        out_specs=(tokens, tokens, P("section", "dp", ("chip", "core"))),
        check_vma=False,
    )
```

```python
import jax
import jax.numpy as jnp
from jax import lax
from jax.sharding import Mesh, PartitionSpec as P

TSTEPS = 4


EPS = 1e-06
THETA = 0.5
SHARP = 4.0


def passed_along(value, axis, steps):
    count = lax.axis_size(axis)
    leading, last = (max(0, -steps), min(count, count - steps))
    return lax.ppermute(value, axis, [(source, source + steps) for source in range(leading, last)])


def lif_rate(gate_act, up_act, leak_rate):
    drive = jax.nn.silu(gate_act) * up_act
    volts = jnp.zeros_like(drive)
    spike_sum = jnp.zeros_like(drive)
    for timestep in range(TSTEPS):
        volts = leak_rate * volts + drive
        spikes = jax.nn.sigmoid(SHARP * (volts - THETA)) - jax.nn.sigmoid(SHARP * (-volts - THETA))
        volts = volts - THETA * spikes
        spike_sum = spike_sum + spikes
    return spike_sum / TSTEPS


def swap_cores(value):
    return lax.ppermute(value, "core", [(0, 1), (1, 0)])


def shifted(value, steps):
    count = lax.axis_size("chip")
    return lax.ppermute(value, "chip", [(source, (source + steps) % count) for source in range(count)])


def to_experts(blocks):
    model_width = blocks.shape[2]
    mine = jnp.stack([blocks[0]] + [shifted(blocks[k], k) for k in range(1, blocks.shape[0])])
    both = jnp.concatenate([mine, swap_cores(mine)], axis=0)
    return both.reshape(-1, model_width)


def from_experts(partials, experts, capacity):
    model_width = partials.shape[1]
    paired = partials.reshape(2, experts, capacity, model_width)
    other = swap_cores(paired[1].astype(jnp.bfloat16))
    summed = (paired[0] + other.astype(jnp.float32)).astype(jnp.bfloat16)
    returned = jnp.stack([summed[0]] + [shifted(summed[k], -k) for k in range(1, experts)])
    return returned.reshape(experts * capacity, model_width).astype(jnp.float32)


def dp_shifted(value, steps):
    count = lax.axis_size("dp")
    return lax.ppermute(value, "dp", [(source, (source + steps) % count) for source in range(count)])


def gather_replicas(piece):
    count = lax.axis_size("dp")
    here = lax.axis_index("dp")
    width = piece.shape[1]
    whole = jnp.zeros((piece.shape[0], width * count), piece.dtype)
    for steps in range(count):
        arrived = piece if steps == 0 else dp_shifted(piece, steps)
        whole = lax.dynamic_update_slice_in_dim(whole, arrived, ((here - steps) % count) * width, 1)
    return whole


def sum_replicas(term):
    count = lax.axis_size("dp")
    here = lax.axis_index("dp")
    rows = term.shape[0] // count
    total = lax.dynamic_slice_in_dim(term, here * rows, rows, 0).astype(jnp.float32)
    for steps in range(1, count):
        chunk = lax.dynamic_slice_in_dim(term, ((here + steps) % count) * rows, rows, 0)
        total = total + dp_shifted(chunk, steps).astype(jnp.float32)
    return total.astype(jnp.bfloat16)


def per_device(
    activations,
    norm_gain,
    route_ids,
    route_gates,
    gate_weight,
    up_weight,
    leak_rates,
    down_weight,
    cotangent,
):
    tok_count = activations.shape[1]
    model_width = activations.shape[2]
    experts = lax.axis_size("chip")
    capacity = min(tok_count, 2 * (9 * tok_count // (8 * experts)))
    tokens = activations[0].astype(jnp.float32)
    gain_row = norm_gain[0]
    inv_rms = lax.rsqrt(jnp.mean(tokens * tokens, axis=-1, keepdims=True) + EPS)
    normed = (tokens * inv_rms * gain_row).astype(jnp.bfloat16)
    flat_ids = (route_ids[0].reshape(-1) - lax.axis_index("chip")) % experts
    onehot = (flat_ids[:, None] == jnp.arange(experts, dtype=jnp.int32)[None, :]).astype(jnp.int32)
    slot_index = jnp.sum(onehot * (jnp.cumsum(onehot, axis=0) - 1), axis=1)
    places = (flat_ids * capacity + slot_index).reshape(tok_count, 2)
    positions = jnp.arange(experts * capacity, dtype=jnp.int32)[:, None]
    pick_first = positions == places[None, :, 0]
    pick_second = positions == places[None, :, 1]
    pick_both = jnp.logical_or(pick_first, pick_second)
    slot_rows = jnp.dot(
        pick_both.astype(jnp.bfloat16), normed, preferred_element_type=jnp.float32
    ).astype(jnp.bfloat16)
    arrived = to_experts(slot_rows.reshape(experts, capacity, model_width))
    gate_local = gate_weight[0]
    up_local = up_weight[0]
    leak_local = leak_rates[0]
    down_full = gather_replicas(down_weight[0])
    gate_act = jnp.dot(arrived, gate_local, preferred_element_type=jnp.float32)
    up_act = jnp.dot(arrived, up_local, preferred_element_type=jnp.float32)
    spike_rate = lif_rate(gate_act, up_act, leak_local).astype(jnp.bfloat16)
    out_part = jnp.dot(spike_rate, down_full, preferred_element_type=jnp.float32)
    expert_out = from_experts(out_part, experts, capacity)
    weights = route_gates[0]
    mixing = jnp.where(pick_first.T, weights[:, 0:1], 0.0) + jnp.where(
        pick_second.T, weights[:, 1:2], 0.0
    )
    moe_sum = jnp.dot(
        mixing, expert_out, precision=lax.Precision.HIGHEST, preferred_element_type=jnp.float32
    )
    section_out = (tokens + moe_sum).astype(jnp.bfloat16)
    passed_on = passed_along(section_out[None], "section", 1)
    upstream = cotangent[0].astype(jnp.float32)
    grad_first = (weights[:, 0:1] * upstream).astype(jnp.bfloat16)
    grad_second = (weights[:, 1:2] * upstream).astype(jnp.bfloat16)
    grad_slots = jnp.dot(
        pick_first.astype(jnp.bfloat16), grad_first, preferred_element_type=jnp.float32
    )
    grad_slots = grad_slots + jnp.dot(
        pick_second.astype(jnp.bfloat16), grad_second, preferred_element_type=jnp.float32
    )
    grad_slots, unused_arrived = lax.optimization_barrier((grad_slots.astype(jnp.bfloat16), arrived))
    grad_rows = to_experts(grad_slots.reshape(experts, capacity, model_width))
    rate_grad = lax.dot_general(
        grad_rows, down_full, (((1,), (1,)), ((), ())), preferred_element_type=jnp.float32
    )
    unused_rate, pullback = jax.vjp(
        lambda gate_in, up_in: lif_rate(gate_in, up_in, leak_local), gate_act, up_act
    )
    gate_grad, up_act_grad = pullback(rate_grad)
    gate_grad = gate_grad.astype(jnp.bfloat16)
    up_act_grad = up_act_grad.astype(jnp.bfloat16)
    back_part = lax.dot_general(
        gate_grad, gate_local, (((1,), (1,)), ((), ())), preferred_element_type=jnp.float32
    )
    back_part = back_part + lax.dot_general(
        up_act_grad, up_local, (((1,), (1,)), ((), ())), preferred_element_type=jnp.float32
    )
    route_back = from_experts(back_part, experts, capacity)
    norm_grad = (
        jnp.dot(
            pick_both.T.astype(jnp.float32),
            route_back,
            precision=lax.Precision.HIGHEST,
            preferred_element_type=jnp.float32,
        )
        * gain_row
    )
    section_back = (
        upstream
        + inv_rms * norm_grad
        - tokens
        * (inv_rms * inv_rms * inv_rms)
        * jnp.mean(tokens * norm_grad, axis=-1, keepdims=True)
    )
    passed_back = passed_along(section_back.astype(jnp.bfloat16)[None], "section", -1)
    up_term = lax.dot_general(
        arrived, up_act_grad, (((0,), (0,)), ((), ())), preferred_element_type=jnp.float32
    )
    up_term = up_term.astype(jnp.bfloat16).astype(jnp.float32)
    up_grad = sum_replicas(up_term.astype(jnp.bfloat16))[None]
    return (passed_on, passed_back, up_grad)


def chip_mesh(mesh):
    sections, replicas, width = mesh.devices.shape
    return Mesh(mesh.devices.reshape(sections, replicas, width // 2, 2), ("section", "dp", "chip", "core"))


def solution(mesh):
    tokens = P("section", ("dp", "chip", "core"), None)
    return jax.shard_map(
        per_device,
        mesh=chip_mesh(mesh),
        in_specs=(
            tokens,
            P("section", None),
            tokens,
            tokens,
            P("section", None, ("chip", "core")),
            P("section", None, ("chip", "core")),
            P("section", ("chip", "core")),
            P("section", ("chip", "core"), "dp"),
            tokens,
        ),
        out_specs=(tokens, tokens, P("section", "dp", ("chip", "core"))),
        check_vma=False,
    )
```

```python
import jax
import jax.numpy as jnp
from jax import lax
from jax.sharding import Mesh, PartitionSpec as P

TSTEPS = 4


EPS = 1e-06
THETA = 0.5
SHARP = 4.0


def passed_along(value, axis, steps):
    count = lax.axis_size(axis)
    leading, last = (max(0, -steps), min(count, count - steps))
    return lax.ppermute(value, axis, [(source, source + steps) for source in range(leading, last)])


def lif_rate(gate_act, up_act, leak_rate):
    drive = jax.nn.silu(gate_act) * up_act
    volts = jnp.zeros_like(drive)
    spike_sum = jnp.zeros_like(drive)
    for timestep in range(TSTEPS):
        volts = leak_rate * volts + drive
        spikes = jax.nn.sigmoid(SHARP * (volts - THETA)) - jax.nn.sigmoid(SHARP * (-volts - THETA))
        volts = volts - THETA * spikes
        spike_sum = spike_sum + spikes
    return spike_sum / TSTEPS


def swap_cores(value):
    return lax.ppermute(value, "core", [(0, 1), (1, 0)])


def shifted(value, steps):
    count = lax.axis_size("chip")
    return lax.ppermute(value, "chip", [(source, (source + steps) % count) for source in range(count)])


def to_experts(blocks):
    model_width = blocks.shape[2]
    mine = jnp.stack([blocks[0]] + [shifted(blocks[k], k) for k in range(1, blocks.shape[0])])
    both = jnp.concatenate([mine, swap_cores(mine)], axis=0)
    return both.reshape(-1, model_width)


def combine_cores(partials, experts, capacity):
    model_width = partials.shape[1]
    paired = partials.reshape(2, experts, capacity, model_width)
    other = swap_cores(paired[1].astype(jnp.bfloat16))
    return (paired[0] + other.astype(jnp.float32)).astype(jnp.bfloat16)


def from_experts(summed):
    experts, capacity, model_width = summed.shape
    returned = jnp.stack([summed[0]] + [shifted(summed[k], -k) for k in range(1, experts)])
    return returned.reshape(experts * capacity, model_width).astype(jnp.float32)


def dp_shifted(value, steps):
    count = lax.axis_size("dp")
    return lax.ppermute(value, "dp", [(source, (source + steps) % count) for source in range(count)])


def gather_replicas(piece):
    count = lax.axis_size("dp")
    here = lax.axis_index("dp")
    width = piece.shape[1]
    whole = jnp.zeros((piece.shape[0], width * count), piece.dtype)
    for steps in range(count):
        arrived = piece if steps == 0 else dp_shifted(piece, steps)
        whole = lax.dynamic_update_slice_in_dim(whole, arrived, ((here - steps) % count) * width, 1)
    return whole


def sum_replicas(term):
    count = lax.axis_size("dp")
    here = lax.axis_index("dp")
    rows = term.shape[0] // count
    total = lax.dynamic_slice_in_dim(term, here * rows, rows, 0).astype(jnp.float32)
    for steps in range(1, count):
        chunk = lax.dynamic_slice_in_dim(term, ((here + steps) % count) * rows, rows, 0)
        total = total + dp_shifted(chunk, steps).astype(jnp.float32)
    return total.astype(jnp.bfloat16)


def per_device(
    activations,
    norm_gain,
    route_ids,
    route_gates,
    gate_weight,
    up_weight,
    leak_rates,
    down_weight,
    cotangent,
):
    tok_count = activations.shape[1]
    model_width = activations.shape[2]
    experts = lax.axis_size("chip")
    capacity = min(tok_count, 2 * (9 * tok_count // (8 * experts)))
    tokens = activations[0].astype(jnp.float32)
    gain_row = norm_gain[0]
    inv_rms = lax.rsqrt(jnp.mean(tokens * tokens, axis=-1, keepdims=True) + EPS)
    normed = (tokens * inv_rms * gain_row).astype(jnp.bfloat16)
    flat_ids = (route_ids[0].reshape(-1) - lax.axis_index("chip")) % experts
    onehot = (flat_ids[:, None] == jnp.arange(experts, dtype=jnp.int32)[None, :]).astype(jnp.int32)
    slot_index = jnp.sum(onehot * (jnp.cumsum(onehot, axis=0) - 1), axis=1)
    places = (flat_ids * capacity + slot_index).reshape(tok_count, 2)
    positions = jnp.arange(experts * capacity, dtype=jnp.int32)[:, None]
    pick_first = positions == places[None, :, 0]
    pick_second = positions == places[None, :, 1]
    pick_both = jnp.logical_or(pick_first, pick_second)
    slot_rows = jnp.dot(
        pick_both.astype(jnp.bfloat16), normed, preferred_element_type=jnp.float32
    ).astype(jnp.bfloat16)
    arrived = to_experts(slot_rows.reshape(experts, capacity, model_width))
    gate_local = gate_weight[0]
    up_local = up_weight[0]
    leak_local = leak_rates[0]
    down_full = gather_replicas(down_weight[0])
    gate_act = jnp.dot(arrived, gate_local, preferred_element_type=jnp.float32)
    up_act = jnp.dot(arrived, up_local, preferred_element_type=jnp.float32)
    spike_rate = lif_rate(gate_act, up_act, leak_local).astype(jnp.bfloat16)
    out_part = jnp.dot(spike_rate, down_full, preferred_element_type=jnp.float32)
    out_summed = combine_cores(out_part, experts, capacity)
    weights = route_gates[0]
    upstream = cotangent[0].astype(jnp.float32)
    grad_first = (weights[:, 0:1] * upstream).astype(jnp.bfloat16)
    grad_second = (weights[:, 1:2] * upstream).astype(jnp.bfloat16)
    grad_slots = jnp.dot(
        pick_first.astype(jnp.bfloat16), grad_first, preferred_element_type=jnp.float32
    )
    grad_slots = grad_slots + jnp.dot(
        pick_second.astype(jnp.bfloat16), grad_second, preferred_element_type=jnp.float32
    )
    grad_slots, unused_arrived = lax.optimization_barrier((grad_slots.astype(jnp.bfloat16), arrived))
    grad_rows = to_experts(grad_slots.reshape(experts, capacity, model_width))
    rate_grad = lax.dot_general(
        grad_rows, down_full, (((1,), (1,)), ((), ())), preferred_element_type=jnp.float32
    )
    unused_rate, pullback = jax.vjp(
        lambda gate_in, up_in: lif_rate(gate_in, up_in, leak_local), gate_act, up_act
    )
    gate_grad, up_act_grad = pullback(rate_grad)
    gate_grad = gate_grad.astype(jnp.bfloat16)
    up_act_grad = up_act_grad.astype(jnp.bfloat16)
    back_part = lax.dot_general(
        gate_grad, gate_local, (((1,), (1,)), ((), ())), preferred_element_type=jnp.float32
    )
    back_part = back_part + lax.dot_general(
        up_act_grad, up_local, (((1,), (1,)), ((), ())), preferred_element_type=jnp.float32
    )
    out_summed, back_summed = lax.optimization_barrier(
        (out_summed, combine_cores(back_part, experts, capacity))
    )
    expert_out = from_experts(out_summed)
    route_back = from_experts(back_summed)
    mixing = jnp.where(pick_first.T, weights[:, 0:1], 0.0) + jnp.where(
        pick_second.T, weights[:, 1:2], 0.0
    )
    moe_sum = jnp.dot(
        mixing, expert_out, precision=lax.Precision.HIGHEST, preferred_element_type=jnp.float32
    )
    section_out = (tokens + moe_sum).astype(jnp.bfloat16)
    passed_on = passed_along(section_out[None], "section", 1)
    norm_grad = (
        jnp.dot(
            pick_both.T.astype(jnp.float32),
            route_back,
            precision=lax.Precision.HIGHEST,
            preferred_element_type=jnp.float32,
        )
        * gain_row
    )
    section_back = (
        upstream
        + inv_rms * norm_grad
        - tokens
        * (inv_rms * inv_rms * inv_rms)
        * jnp.mean(tokens * norm_grad, axis=-1, keepdims=True)
    )
    passed_back = passed_along(section_back.astype(jnp.bfloat16)[None], "section", -1)
    up_term = lax.dot_general(
        arrived, up_act_grad, (((0,), (0,)), ((), ())), preferred_element_type=jnp.float32
    )
    up_term = up_term.astype(jnp.bfloat16).astype(jnp.float32)
    up_grad = sum_replicas(up_term.astype(jnp.bfloat16))[None]
    return (passed_on, passed_back, up_grad)


def chip_mesh(mesh):
    sections, replicas, width = mesh.devices.shape
    return Mesh(mesh.devices.reshape(sections, replicas, width // 2, 2), ("section", "dp", "chip", "core"))


def solution(mesh):
    tokens = P("section", ("dp", "chip", "core"), None)
    return jax.shard_map(
        per_device,
        mesh=chip_mesh(mesh),
        in_specs=(
            tokens,
            P("section", None),
            tokens,
            tokens,
            P("section", None, ("chip", "core")),
            P("section", None, ("chip", "core")),
            P("section", ("chip", "core")),
            P("section", ("chip", "core"), "dp"),
            tokens,
        ),
        out_specs=(tokens, tokens, P("section", "dp", ("chip", "core"))),
        check_vma=False,
    )
```

```python
import jax
import jax.numpy as jnp
from jax import lax
from jax.sharding import Mesh, PartitionSpec as P

TSTEPS = 4


EPS = 1e-06
THETA = 0.5
SHARP = 4.0


def passed_along(value, axis, steps):
    count = lax.axis_size(axis)
    leading, last = (max(0, -steps), min(count, count - steps))
    return lax.ppermute(value, axis, [(source, source + steps) for source in range(leading, last)])


def lif_rate(gate_act, up_act, leak_rate):
    drive = jax.nn.silu(gate_act) * up_act
    volts = jnp.zeros_like(drive)
    spike_sum = jnp.zeros_like(drive)
    for timestep in range(TSTEPS):
        volts = leak_rate * volts + drive
        spikes = jax.nn.sigmoid(SHARP * (volts - THETA)) - jax.nn.sigmoid(SHARP * (-volts - THETA))
        volts = volts - THETA * spikes
        spike_sum = spike_sum + spikes
    return spike_sum / TSTEPS


def swap_cores(value):
    return lax.ppermute(value, "core", [(0, 1), (1, 0)])


def shifted(value, steps):
    count = lax.axis_size("chip")
    return lax.ppermute(value, "chip", [(source, (source + steps) % count) for source in range(count)])


def to_experts(blocks):
    model_width = blocks.shape[2]
    mine = jnp.stack([blocks[0]] + [shifted(blocks[k], k) for k in range(1, blocks.shape[0])])
    both = jnp.concatenate([mine, swap_cores(mine)], axis=0)
    return both.reshape(-1, model_width)


def combine_cores(partials, experts, capacity):
    model_width = partials.shape[1]
    paired = partials.reshape(2, experts, capacity, model_width)
    other = swap_cores(paired[1].astype(jnp.bfloat16))
    return (paired[0] + other.astype(jnp.float32)).astype(jnp.bfloat16)


def from_experts(summed):
    experts, capacity, model_width = summed.shape
    returned = jnp.stack([summed[0]] + [shifted(summed[k], -k) for k in range(1, experts)])
    return returned.reshape(experts * capacity, model_width).astype(jnp.float32)


def dp_shifted(value, steps):
    count = lax.axis_size("dp")
    return lax.ppermute(value, "dp", [(source, (source + steps) % count) for source in range(count)])


def gather_replicas(piece):
    count = lax.axis_size("dp")
    here = lax.axis_index("dp")
    width = piece.shape[1]
    whole = jnp.zeros((piece.shape[0], width * count), piece.dtype)
    for steps in range(count):
        arrived = piece if steps == 0 else dp_shifted(piece, steps)
        whole = lax.dynamic_update_slice_in_dim(whole, arrived, ((here - steps) % count) * width, 1)
    return whole


def sum_replicas(term):
    count = lax.axis_size("dp")
    here = lax.axis_index("dp")
    rows = term.shape[0] // count
    total = lax.dynamic_slice_in_dim(term, here * rows, rows, 0).astype(jnp.float32)
    for steps in range(1, count):
        chunk = lax.dynamic_slice_in_dim(term, ((here + steps) % count) * rows, rows, 0)
        total = total + dp_shifted(chunk, steps).astype(jnp.float32)
    return total.astype(jnp.bfloat16)


def per_device(
    activations,
    norm_gain,
    route_ids,
    route_gates,
    gate_weight,
    up_weight,
    leak_rates,
    down_weight,
    cotangent,
):
    tok_count = activations.shape[1]
    model_width = activations.shape[2]
    experts = lax.axis_size("chip")
    capacity = min(tok_count, 2 * (9 * tok_count // (8 * experts)))
    tokens = activations[0].astype(jnp.float32)
    gain_row = norm_gain[0]
    inv_rms = lax.rsqrt(jnp.mean(tokens * tokens, axis=-1, keepdims=True) + EPS)
    normed = (tokens * inv_rms * gain_row).astype(jnp.bfloat16)
    flat_ids = (route_ids[0].reshape(-1) - lax.axis_index("chip")) % experts
    onehot = (flat_ids[:, None] == jnp.arange(experts, dtype=jnp.int32)[None, :]).astype(jnp.int32)
    slot_index = jnp.sum(onehot * (jnp.cumsum(onehot, axis=0) - 1), axis=1)
    places = (flat_ids * capacity + slot_index).reshape(tok_count, 2)
    positions = jnp.arange(experts * capacity, dtype=jnp.int32)[:, None]
    pick_first = positions == places[None, :, 0]
    pick_second = positions == places[None, :, 1]
    pick_both = jnp.logical_or(pick_first, pick_second)
    slot_rows = jnp.dot(
        pick_both.astype(jnp.bfloat16), normed, preferred_element_type=jnp.float32
    ).astype(jnp.bfloat16)
    arrived = to_experts(slot_rows.reshape(experts, capacity, model_width))
    gate_local = gate_weight[0]
    up_local = up_weight[0]
    leak_local = leak_rates[0]
    down_full = gather_replicas(down_weight[0])
    gate_act = jnp.dot(arrived, gate_local, preferred_element_type=jnp.float32)
    up_act = jnp.dot(arrived, up_local, preferred_element_type=jnp.float32)
    spike_rate = lif_rate(gate_act, up_act, leak_local).astype(jnp.bfloat16)
    out_part = jnp.dot(spike_rate, down_full, preferred_element_type=jnp.float32)
    out_summed = combine_cores(out_part, experts, capacity)
    weights = route_gates[0]
    upstream = cotangent[0].astype(jnp.float32)
    grad_first = (weights[:, 0:1] * upstream).astype(jnp.bfloat16)
    grad_second = (weights[:, 1:2] * upstream).astype(jnp.bfloat16)
    grad_slots = jnp.dot(
        pick_first.astype(jnp.bfloat16), grad_first, preferred_element_type=jnp.float32
    )
    grad_slots = grad_slots + jnp.dot(
        pick_second.astype(jnp.bfloat16), grad_second, preferred_element_type=jnp.float32
    )
    grad_slots, unused_arrived = lax.optimization_barrier((grad_slots.astype(jnp.bfloat16), arrived))
    grad_rows = to_experts(grad_slots.reshape(experts, capacity, model_width))
    rate_grad = lax.dot_general(
        grad_rows, down_full, (((1,), (1,)), ((), ())), preferred_element_type=jnp.float32
    )
    unused_rate, pullback = jax.vjp(
        lambda gate_in, up_in: lif_rate(gate_in, up_in, leak_local), gate_act, up_act
    )
    gate_grad, up_act_grad = pullback(rate_grad)
    gate_grad = gate_grad.astype(jnp.bfloat16)
    up_act_grad = up_act_grad.astype(jnp.bfloat16)
    back_part = lax.dot_general(
        gate_grad, gate_local, (((1,), (1,)), ((), ())), preferred_element_type=jnp.float32
    )
    back_part = back_part + lax.dot_general(
        up_act_grad, up_local, (((1,), (1,)), ((), ())), preferred_element_type=jnp.float32
    )
    out_summed, back_summed = lax.optimization_barrier(
        (out_summed, combine_cores(back_part, experts, capacity))
    )
    expert_out = from_experts(out_summed)
    back_summed, expert_out = lax.optimization_barrier((back_summed, expert_out))
    route_back = from_experts(back_summed)
    mixing = jnp.where(pick_first.T, weights[:, 0:1], 0.0) + jnp.where(
        pick_second.T, weights[:, 1:2], 0.0
    )
    moe_sum = jnp.dot(
        mixing, expert_out, precision=lax.Precision.HIGHEST, preferred_element_type=jnp.float32
    )
    section_out = (tokens + moe_sum).astype(jnp.bfloat16)
    passed_on = passed_along(section_out[None], "section", 1)
    norm_grad = (
        jnp.dot(
            pick_both.T.astype(jnp.float32),
            route_back,
            precision=lax.Precision.HIGHEST,
            preferred_element_type=jnp.float32,
        )
        * gain_row
    )
    section_back = (
        upstream
        + inv_rms * norm_grad
        - tokens
        * (inv_rms * inv_rms * inv_rms)
        * jnp.mean(tokens * norm_grad, axis=-1, keepdims=True)
    )
    passed_back = passed_along(section_back.astype(jnp.bfloat16)[None], "section", -1)
    up_term = lax.dot_general(
        arrived, up_act_grad, (((0,), (0,)), ((), ())), preferred_element_type=jnp.float32
    )
    up_term = up_term.astype(jnp.bfloat16).astype(jnp.float32)
    up_grad = sum_replicas(up_term.astype(jnp.bfloat16))[None]
    return (passed_on, passed_back, up_grad)


def chip_mesh(mesh):
    sections, replicas, width = mesh.devices.shape
    return Mesh(mesh.devices.reshape(sections, replicas, width // 2, 2), ("section", "dp", "chip", "core"))


def solution(mesh):
    tokens = P("section", ("dp", "chip", "core"), None)
    return jax.shard_map(
        per_device,
        mesh=chip_mesh(mesh),
        in_specs=(
            tokens,
            P("section", None),
            tokens,
            tokens,
            P("section", None, ("chip", "core")),
            P("section", None, ("chip", "core")),
            P("section", ("chip", "core")),
            P("section", ("chip", "core"), "dp"),
            tokens,
        ),
        out_specs=(tokens, tokens, P("section", "dp", ("chip", "core"))),
        check_vma=False,
    )
```

```python
import jax
import jax.numpy as jnp
from jax import lax
from jax.sharding import Mesh, PartitionSpec as P

TSTEPS = 4


EPS = 1e-06
THETA = 0.5
SHARP = 4.0


def passed_along(value, axis, steps):
    count = lax.axis_size(axis)
    leading, last = (max(0, -steps), min(count, count - steps))
    return lax.ppermute(value, axis, [(source, source + steps) for source in range(leading, last)])


def lif_rate(gate_act, up_act, leak_rate):
    drive = jax.nn.silu(gate_act) * up_act
    volts = jnp.zeros_like(drive)
    spike_sum = jnp.zeros_like(drive)
    for timestep in range(TSTEPS):
        volts = leak_rate * volts + drive
        spikes = jax.nn.sigmoid(SHARP * (volts - THETA)) - jax.nn.sigmoid(SHARP * (-volts - THETA))
        volts = volts - THETA * spikes
        spike_sum = spike_sum + spikes
    return spike_sum / TSTEPS


def swap_cores(value):
    return lax.ppermute(value, "core", [(0, 1), (1, 0)])


def shifted(value, steps):
    count = lax.axis_size("chip")
    return lax.ppermute(value, "chip", [(source, (source + steps) % count) for source in range(count)])


def to_experts(blocks):
    model_width = blocks.shape[2]
    mine = jnp.stack([blocks[0]] + [shifted(blocks[k], k) for k in range(1, blocks.shape[0])])
    both = jnp.concatenate([mine, swap_cores(mine)], axis=0)
    return both.reshape(-1, model_width)


def combine_cores(partials, experts, capacity):
    model_width = partials.shape[1]
    paired = partials.reshape(2, experts, capacity, model_width)
    other = swap_cores(paired[1].astype(jnp.bfloat16))
    return (paired[0] + other.astype(jnp.float32)).astype(jnp.bfloat16)


def from_experts(summed):
    experts, capacity, model_width = summed.shape
    returned = jnp.stack([summed[0]] + [shifted(summed[k], -k) for k in range(1, experts)])
    return returned.reshape(experts * capacity, model_width).astype(jnp.float32)


def dp_shifted(value, steps):
    count = lax.axis_size("dp")
    return lax.ppermute(value, "dp", [(source, (source + steps) % count) for source in range(count)])


def gather_replicas(piece):
    count = lax.axis_size("dp")
    here = lax.axis_index("dp")
    width = piece.shape[1]
    whole = jnp.zeros((piece.shape[0], width * count), piece.dtype)
    for steps in range(count):
        arrived = piece if steps == 0 else dp_shifted(piece, steps)
        whole = lax.dynamic_update_slice_in_dim(whole, arrived, ((here - steps) % count) * width, 1)
    return whole


def sum_replicas(term):
    count = lax.axis_size("dp")
    here = lax.axis_index("dp")
    rows = term.shape[0] // count
    total = lax.dynamic_slice_in_dim(term, here * rows, rows, 0).astype(jnp.float32)
    for steps in range(1, count):
        chunk = lax.dynamic_slice_in_dim(term, ((here + steps) % count) * rows, rows, 0)
        total = total + dp_shifted(chunk, steps).astype(jnp.float32)
    return total.astype(jnp.bfloat16)


def per_device(
    activations,
    norm_gain,
    route_ids,
    route_gates,
    gate_weight,
    up_weight,
    leak_rates,
    down_weight,
    cotangent,
):
    tok_count = activations.shape[1]
    model_width = activations.shape[2]
    experts = lax.axis_size("chip")
    capacity = min(tok_count, 2 * (9 * tok_count // (8 * experts)))
    tokens = activations[0].astype(jnp.float32)
    gain_row = norm_gain[0]
    inv_rms = lax.rsqrt(jnp.mean(tokens * tokens, axis=-1, keepdims=True) + EPS)
    normed = (tokens * inv_rms * gain_row).astype(jnp.bfloat16)
    flat_ids = (route_ids[0].reshape(-1) - lax.axis_index("chip")) % experts
    onehot = (flat_ids[:, None] == jnp.arange(experts, dtype=jnp.int32)[None, :]).astype(jnp.int32)
    slot_index = jnp.sum(onehot * (jnp.cumsum(onehot, axis=0) - 1), axis=1)
    places = (flat_ids * capacity + slot_index).reshape(tok_count, 2)
    positions = jnp.arange(experts * capacity, dtype=jnp.int32)[:, None]
    pick_first = positions == places[None, :, 0]
    pick_second = positions == places[None, :, 1]
    pick_both = jnp.logical_or(pick_first, pick_second)
    slot_rows = jnp.dot(
        pick_both.astype(jnp.bfloat16), normed, preferred_element_type=jnp.float32
    ).astype(jnp.bfloat16)
    arrived = to_experts(slot_rows.reshape(experts, capacity, model_width))
    gate_local = gate_weight[0]
    up_local = up_weight[0]
    leak_local = leak_rates[0]
    down_full = gather_replicas(down_weight[0])
    gate_act = jnp.dot(arrived, gate_local, preferred_element_type=jnp.float32)
    up_act = jnp.dot(arrived, up_local, preferred_element_type=jnp.float32)
    spike_rate = lif_rate(gate_act, up_act, leak_local).astype(jnp.bfloat16)
    out_part = jnp.dot(spike_rate, down_full, preferred_element_type=jnp.float32)
    out_summed = combine_cores(out_part, experts, capacity)
    weights = route_gates[0]
    upstream = cotangent[0].astype(jnp.float32)
    grad_first = (weights[:, 0:1] * upstream).astype(jnp.bfloat16)
    grad_second = (weights[:, 1:2] * upstream).astype(jnp.bfloat16)
    grad_slots = jnp.dot(
        pick_first.astype(jnp.bfloat16), grad_first, preferred_element_type=jnp.float32
    )
    grad_slots = grad_slots + jnp.dot(
        pick_second.astype(jnp.bfloat16), grad_second, preferred_element_type=jnp.float32
    )
    grad_slots, unused_arrived = lax.optimization_barrier((grad_slots.astype(jnp.bfloat16), arrived))
    grad_rows = to_experts(grad_slots.reshape(experts, capacity, model_width))
    rate_grad = lax.dot_general(
        grad_rows, down_full, (((1,), (1,)), ((), ())), preferred_element_type=jnp.float32
    )
    unused_rate, pullback = jax.vjp(
        lambda gate_in, up_in: lif_rate(gate_in, up_in, leak_local), gate_act, up_act
    )
    gate_grad, up_act_grad = pullback(rate_grad)
    gate_grad = gate_grad.astype(jnp.bfloat16)
    up_act_grad = up_act_grad.astype(jnp.bfloat16)
    back_part = lax.dot_general(
        gate_grad, gate_local, (((1,), (1,)), ((), ())), preferred_element_type=jnp.float32
    )
    back_part = back_part + lax.dot_general(
        up_act_grad, up_local, (((1,), (1,)), ((), ())), preferred_element_type=jnp.float32
    )
    out_summed, back_summed = lax.optimization_barrier(
        (out_summed, combine_cores(back_part, experts, capacity))
    )
    expert_out = from_experts(out_summed)
    back_summed, expert_out = lax.optimization_barrier((back_summed, expert_out))
    route_back = from_experts(back_summed)
    moe_sum = weights[:, 0:1] * jnp.take(expert_out, places[:, 0], axis=0) + weights[
        :, 1:2
    ] * jnp.take(expert_out, places[:, 1], axis=0)
    section_out = (tokens + moe_sum).astype(jnp.bfloat16)
    passed_on = passed_along(section_out[None], "section", 1)
    norm_grad = (
        jnp.take(route_back, places[:, 0], axis=0) + jnp.take(route_back, places[:, 1], axis=0)
    ) * gain_row
    section_back = (
        upstream
        + inv_rms * norm_grad
        - tokens
        * (inv_rms * inv_rms * inv_rms)
        * jnp.mean(tokens * norm_grad, axis=-1, keepdims=True)
    )
    passed_back = passed_along(section_back.astype(jnp.bfloat16)[None], "section", -1)
    up_term = lax.dot_general(
        arrived, up_act_grad, (((0,), (0,)), ((), ())), preferred_element_type=jnp.float32
    )
    up_term = up_term.astype(jnp.bfloat16).astype(jnp.float32)
    up_grad = sum_replicas(up_term.astype(jnp.bfloat16))[None]
    return (passed_on, passed_back, up_grad)


def chip_mesh(mesh):
    sections, replicas, width = mesh.devices.shape
    return Mesh(mesh.devices.reshape(sections, replicas, width // 2, 2), ("section", "dp", "chip", "core"))


def solution(mesh):
    tokens = P("section", ("dp", "chip", "core"), None)
    return jax.shard_map(
        per_device,
        mesh=chip_mesh(mesh),
        in_specs=(
            tokens,
            P("section", None),
            tokens,
            tokens,
            P("section", None, ("chip", "core")),
            P("section", None, ("chip", "core")),
            P("section", ("chip", "core")),
            P("section", ("chip", "core"), "dp"),
            tokens,
        ),
        out_specs=(tokens, tokens, P("section", "dp", ("chip", "core"))),
        check_vma=False,
    )
```

```python
import jax
import jax.numpy as jnp
from jax import lax
from jax.sharding import Mesh, PartitionSpec as P

TSTEPS = 4


EPS = 1e-06
THETA = 0.5
SHARP = 4.0


def passed_along(value, axis, steps):
    count = lax.axis_size(axis)
    leading, last = (max(0, -steps), min(count, count - steps))
    moved = lax.ppermute(value, axis, [(source, source + steps) for source in range(leading, last)])
    receiver = lax.axis_index(axis)
    has_source = jnp.logical_and(receiver - steps >= 0, receiver - steps < count)
    return jnp.where(has_source, moved, jnp.zeros_like(moved))


def lif_rate(gate_act, up_act, leak_rate):
    drive = jax.nn.silu(gate_act) * up_act
    volts = jnp.zeros_like(drive)
    spike_sum = jnp.zeros_like(drive)
    for timestep in range(TSTEPS):
        volts = leak_rate * volts + drive
        spikes = jax.nn.sigmoid(SHARP * (volts - THETA)) - jax.nn.sigmoid(SHARP * (-volts - THETA))
        volts = volts - THETA * spikes
        spike_sum = spike_sum + spikes
    return spike_sum / TSTEPS


def swap_cores(value):
    return lax.ppermute(value, "core", [(0, 1), (1, 0)])


def shifted(value, steps):
    count = lax.axis_size("chip")
    return lax.ppermute(value, "chip", [(source, (source + steps) % count) for source in range(count)])


def to_experts(blocks):
    model_width = blocks.shape[2]
    mine = jnp.stack([blocks[0]] + [shifted(blocks[k], k) for k in range(1, blocks.shape[0])])
    both = jnp.concatenate([mine, swap_cores(mine)], axis=0)
    return both.reshape(-1, model_width)


def combine_cores(partials, experts, capacity):
    model_width = partials.shape[1]
    paired = partials.reshape(2, experts, capacity, model_width)
    other = swap_cores(paired[1].astype(jnp.bfloat16))
    return (paired[0] + other.astype(jnp.float32)).astype(jnp.bfloat16)


def from_experts(summed):
    experts, capacity, model_width = summed.shape
    returned = jnp.stack([summed[0]] + [shifted(summed[k], -k) for k in range(1, experts)])
    return returned.reshape(experts * capacity, model_width).astype(jnp.float32)


def dp_shifted(value, steps):
    count = lax.axis_size("dp")
    return lax.ppermute(value, "dp", [(source, (source + steps) % count) for source in range(count)])


def gather_replicas(piece):
    count = lax.axis_size("dp")
    here = lax.axis_index("dp")
    width = piece.shape[1]
    whole = jnp.zeros((piece.shape[0], width * count), piece.dtype)
    for steps in range(count):
        arrived = piece if steps == 0 else dp_shifted(piece, steps)
        whole = lax.dynamic_update_slice_in_dim(whole, arrived, ((here - steps) % count) * width, 1)
    return whole


def sum_replicas(term):
    count = lax.axis_size("dp")
    here = lax.axis_index("dp")
    rows = term.shape[0] // count
    total = lax.dynamic_slice_in_dim(term, here * rows, rows, 0).astype(jnp.float32)
    for steps in range(1, count):
        chunk = lax.dynamic_slice_in_dim(term, ((here + steps) % count) * rows, rows, 0)
        total = total + dp_shifted(chunk, steps).astype(jnp.float32)
    return total.astype(jnp.bfloat16)


def per_device(
    activations,
    norm_gain,
    route_ids,
    route_gates,
    gate_weight,
    up_weight,
    leak_rates,
    down_weight,
    cotangent,
):
    tok_count = activations.shape[1]
    model_width = activations.shape[2]
    experts = lax.axis_size("chip")
    capacity = min(tok_count, 2 * (9 * tok_count // (8 * experts)))
    tokens = activations[0].astype(jnp.float32)
    gain_row = norm_gain[0]
    inv_rms = lax.rsqrt(jnp.mean(tokens * tokens, axis=-1, keepdims=True) + EPS)
    normed = (tokens * inv_rms * gain_row).astype(jnp.bfloat16)
    flat_ids = (route_ids[0].reshape(-1) - lax.axis_index("chip")) % experts
    onehot = (flat_ids[:, None] == jnp.arange(experts, dtype=jnp.int32)[None, :]).astype(jnp.int32)
    slot_index = jnp.sum(onehot * (jnp.cumsum(onehot, axis=0) - 1), axis=1)
    places = (flat_ids * capacity + slot_index).reshape(tok_count, 2)
    positions = jnp.arange(experts * capacity, dtype=jnp.int32)[:, None]
    pick_first = positions == places[None, :, 0]
    pick_second = positions == places[None, :, 1]
    pick_both = jnp.logical_or(pick_first, pick_second)
    slot_rows = jnp.dot(
        pick_both.astype(jnp.bfloat16), normed, preferred_element_type=jnp.float32
    ).astype(jnp.bfloat16)
    arrived = to_experts(slot_rows.reshape(experts, capacity, model_width))
    gate_local = gate_weight[0]
    up_local = up_weight[0]
    leak_local = leak_rates[0]
    down_full = gather_replicas(down_weight[0])
    gate_act = jnp.dot(arrived, gate_local, preferred_element_type=jnp.float32)
    up_act = jnp.dot(arrived, up_local, preferred_element_type=jnp.float32)
    spike_rate = lif_rate(gate_act, up_act, leak_local).astype(jnp.bfloat16)
    out_part = jnp.dot(spike_rate, down_full, preferred_element_type=jnp.float32)
    out_summed = combine_cores(out_part, experts, capacity)
    weights = route_gates[0]
    upstream = cotangent[0].astype(jnp.float32)
    grad_first = (weights[:, 0:1] * upstream).astype(jnp.bfloat16)
    grad_second = (weights[:, 1:2] * upstream).astype(jnp.bfloat16)
    grad_slots = jnp.dot(
        pick_first.astype(jnp.bfloat16), grad_first, preferred_element_type=jnp.float32
    )
    grad_slots = grad_slots + jnp.dot(
        pick_second.astype(jnp.bfloat16), grad_second, preferred_element_type=jnp.float32
    )
    grad_slots, unused_arrived = lax.optimization_barrier((grad_slots.astype(jnp.bfloat16), arrived))
    grad_rows = to_experts(grad_slots.reshape(experts, capacity, model_width))
    rate_grad = lax.dot_general(
        grad_rows, down_full, (((1,), (1,)), ((), ())), preferred_element_type=jnp.float32
    )
    unused_rate, pullback = jax.vjp(
        lambda gate_in, up_in: lif_rate(gate_in, up_in, leak_local), gate_act, up_act
    )
    gate_grad, up_act_grad = pullback(rate_grad)
    gate_grad = gate_grad.astype(jnp.bfloat16)
    up_act_grad = up_act_grad.astype(jnp.bfloat16)
    back_part = lax.dot_general(
        gate_grad, gate_local, (((1,), (1,)), ((), ())), preferred_element_type=jnp.float32
    )
    back_part = back_part + lax.dot_general(
        up_act_grad, up_local, (((1,), (1,)), ((), ())), preferred_element_type=jnp.float32
    )
    out_summed, back_summed = lax.optimization_barrier(
        (out_summed, combine_cores(back_part, experts, capacity))
    )
    expert_out = from_experts(out_summed)
    back_summed, expert_out = lax.optimization_barrier((back_summed, expert_out))
    route_back = from_experts(back_summed)
    mixing = jnp.where(pick_first.T, weights[:, 0:1], 0.0) + jnp.where(
        pick_second.T, weights[:, 1:2], 0.0
    )
    moe_sum = jnp.dot(
        mixing, expert_out, precision=lax.Precision.HIGHEST, preferred_element_type=jnp.float32
    )
    section_out = (tokens + moe_sum).astype(jnp.bfloat16)
    passed_on = passed_along(section_out[None], "section", 1)
    norm_grad = (
        jnp.dot(
            pick_both.T.astype(jnp.float32),
            route_back,
            precision=lax.Precision.HIGHEST,
            preferred_element_type=jnp.float32,
        )
        * gain_row
    )
    section_back = (
        upstream
        + inv_rms * norm_grad
        - tokens
        * (inv_rms * inv_rms * inv_rms)
        * jnp.mean(tokens * norm_grad, axis=-1, keepdims=True)
    )
    passed_back = passed_along(section_back.astype(jnp.bfloat16)[None], "section", -1)
    up_term = lax.dot_general(
        arrived, up_act_grad, (((0,), (0,)), ((), ())), preferred_element_type=jnp.float32
    )
    up_term = up_term.astype(jnp.bfloat16).astype(jnp.float32)
    up_grad = sum_replicas(up_term.astype(jnp.bfloat16))[None]
    return (passed_on, passed_back, up_grad)


def chip_mesh(mesh):
    sections, replicas, width = mesh.devices.shape
    return Mesh(mesh.devices.reshape(sections, replicas, width // 2, 2), ("section", "dp", "chip", "core"))


def solution(mesh):
    tokens = P("section", ("dp", "chip", "core"), None)
    return jax.shard_map(
        per_device,
        mesh=chip_mesh(mesh),
        in_specs=(
            tokens,
            P("section", None),
            tokens,
            tokens,
            P("section", None, ("chip", "core")),
            P("section", None, ("chip", "core")),
            P("section", ("chip", "core")),
            P("section", ("chip", "core"), "dp"),
            tokens,
        ),
        out_specs=(tokens, tokens, P("section", "dp", ("chip", "core"))),
        check_vma=False,
    )
```

```python
import jax
import jax.numpy as jnp
from jax import lax
from jax.sharding import Mesh, PartitionSpec as P

TSTEPS = 4


EPS = 1e-06
THETA = 0.5
SHARP = 4.0


def passed_along(value, axis, steps):
    count = lax.axis_size(axis)
    leading, last = (max(0, -steps), min(count, count - steps))
    moved = lax.ppermute(value, axis, [(source, source + steps) for source in range(leading, last)])
    receiver = lax.axis_index(axis)
    has_source = jnp.logical_and(receiver - steps >= 0, receiver - steps < count)
    return jnp.where(has_source, moved, jnp.zeros_like(moved))


def lif_rate(gate_act, up_act, leak_rate):
    drive = jax.nn.silu(gate_act) * up_act
    volts = jnp.zeros_like(drive)
    spike_sum = jnp.zeros_like(drive)
    for timestep in range(TSTEPS):
        volts = leak_rate * volts + drive
        spikes = jax.nn.sigmoid(SHARP * (volts - THETA)) - jax.nn.sigmoid(SHARP * (-volts - THETA))
        volts = volts - THETA * spikes
        spike_sum = spike_sum + spikes
    return spike_sum / TSTEPS


def swap_cores(value):
    return lax.ppermute(value, "core", [(0, 1), (1, 0)])


def shifted(value, steps):
    count = lax.axis_size("chip")
    return lax.ppermute(value, "chip", [(source, (source + steps) % count) for source in range(count)])


def to_experts(blocks):
    model_width = blocks.shape[2]
    received = [blocks[0]] + [shifted(blocks[k], k) for k in range(1, blocks.shape[0])]
    both = jnp.stack(received + [swap_cores(block) for block in received])
    return both.reshape(-1, model_width)


def combine_cores(partials, experts, capacity):
    model_width = partials.shape[1]
    paired = partials.reshape(2, experts, capacity, model_width)
    other = swap_cores(paired[1].astype(jnp.bfloat16))
    return (paired[0] + other.astype(jnp.float32)).astype(jnp.bfloat16)


def from_experts(summed):
    experts, capacity, model_width = summed.shape
    returned = jnp.stack([summed[0]] + [shifted(summed[k], -k) for k in range(1, experts)])
    return returned.reshape(experts * capacity, model_width).astype(jnp.float32)


def dp_shifted(value, steps):
    count = lax.axis_size("dp")
    return lax.ppermute(value, "dp", [(source, (source + steps) % count) for source in range(count)])


def gather_replicas(piece):
    count = lax.axis_size("dp")
    here = lax.axis_index("dp")
    width = piece.shape[1]
    whole = jnp.zeros((piece.shape[0], width * count), piece.dtype)
    for steps in range(count):
        arrived = piece if steps == 0 else dp_shifted(piece, steps)
        whole = lax.dynamic_update_slice_in_dim(whole, arrived, ((here - steps) % count) * width, 1)
    return whole


def sum_replicas(term):
    count = lax.axis_size("dp")
    here = lax.axis_index("dp")
    rows = term.shape[0] // count
    total = lax.dynamic_slice_in_dim(term, here * rows, rows, 0).astype(jnp.float32)
    for steps in range(1, count):
        chunk = lax.dynamic_slice_in_dim(term, ((here + steps) % count) * rows, rows, 0)
        total = total + dp_shifted(chunk, steps).astype(jnp.float32)
    return total.astype(jnp.bfloat16)


def per_device(
    activations,
    norm_gain,
    route_ids,
    route_gates,
    gate_weight,
    up_weight,
    leak_rates,
    down_weight,
    cotangent,
):
    tok_count = activations.shape[1]
    model_width = activations.shape[2]
    experts = lax.axis_size("chip")
    capacity = min(tok_count, 2 * (9 * tok_count // (8 * experts)))
    tokens = activations[0].astype(jnp.float32)
    gain_row = norm_gain[0]
    inv_rms = lax.rsqrt(jnp.mean(tokens * tokens, axis=-1, keepdims=True) + EPS)
    normed = (tokens * inv_rms * gain_row).astype(jnp.bfloat16)
    flat_ids = (route_ids[0].reshape(-1) - lax.axis_index("chip")) % experts
    onehot = (flat_ids[:, None] == jnp.arange(experts, dtype=jnp.int32)[None, :]).astype(jnp.int32)
    slot_index = jnp.sum(onehot * (jnp.cumsum(onehot, axis=0) - 1), axis=1)
    places = (flat_ids * capacity + slot_index).reshape(tok_count, 2)
    positions = jnp.arange(experts * capacity, dtype=jnp.int32)[:, None]
    pick_first = positions == places[None, :, 0]
    pick_second = positions == places[None, :, 1]
    pick_both = jnp.logical_or(pick_first, pick_second)
    slot_rows = jnp.dot(
        pick_both.astype(jnp.bfloat16), normed, preferred_element_type=jnp.float32
    ).astype(jnp.bfloat16)
    arrived = to_experts(slot_rows.reshape(experts, capacity, model_width))
    gate_local = gate_weight[0]
    up_local = up_weight[0]
    leak_local = leak_rates[0]
    down_full = gather_replicas(down_weight[0])
    gate_act = jnp.dot(arrived, gate_local, preferred_element_type=jnp.float32)
    up_act = jnp.dot(arrived, up_local, preferred_element_type=jnp.float32)
    spike_rate = lif_rate(gate_act, up_act, leak_local).astype(jnp.bfloat16)
    out_part = jnp.dot(spike_rate, down_full, preferred_element_type=jnp.float32)
    out_summed = combine_cores(out_part, experts, capacity)
    weights = route_gates[0]
    upstream = cotangent[0].astype(jnp.float32)
    grad_first = (weights[:, 0:1] * upstream).astype(jnp.bfloat16)
    grad_second = (weights[:, 1:2] * upstream).astype(jnp.bfloat16)
    grad_slots = jnp.dot(
        pick_first.astype(jnp.bfloat16), grad_first, preferred_element_type=jnp.float32
    )
    grad_slots = grad_slots + jnp.dot(
        pick_second.astype(jnp.bfloat16), grad_second, preferred_element_type=jnp.float32
    )
    grad_slots, unused_arrived = lax.optimization_barrier((grad_slots.astype(jnp.bfloat16), arrived))
    grad_rows = to_experts(grad_slots.reshape(experts, capacity, model_width))
    rate_grad = lax.dot_general(
        grad_rows, down_full, (((1,), (1,)), ((), ())), preferred_element_type=jnp.float32
    )
    unused_rate, pullback = jax.vjp(
        lambda gate_in, up_in: lif_rate(gate_in, up_in, leak_local), gate_act, up_act
    )
    gate_grad, up_act_grad = pullback(rate_grad)
    gate_grad = gate_grad.astype(jnp.bfloat16)
    up_act_grad = up_act_grad.astype(jnp.bfloat16)
    back_part = lax.dot_general(
        gate_grad, gate_local, (((1,), (1,)), ((), ())), preferred_element_type=jnp.float32
    )
    back_part = back_part + lax.dot_general(
        up_act_grad, up_local, (((1,), (1,)), ((), ())), preferred_element_type=jnp.float32
    )
    out_summed, back_summed = lax.optimization_barrier(
        (out_summed, combine_cores(back_part, experts, capacity))
    )
    expert_out = from_experts(out_summed)
    back_summed, expert_out = lax.optimization_barrier((back_summed, expert_out))
    route_back = from_experts(back_summed)
    mixing = jnp.where(pick_first.T, weights[:, 0:1], 0.0) + jnp.where(
        pick_second.T, weights[:, 1:2], 0.0
    )
    moe_sum = jnp.dot(
        mixing, expert_out, precision=lax.Precision.HIGHEST, preferred_element_type=jnp.float32
    )
    section_out = (tokens + moe_sum).astype(jnp.bfloat16)
    passed_on = passed_along(section_out[None], "section", 1)
    norm_grad = (
        jnp.dot(
            pick_both.T.astype(jnp.float32),
            route_back,
            precision=lax.Precision.HIGHEST,
            preferred_element_type=jnp.float32,
        )
        * gain_row
    )
    section_back = (
        upstream
        + inv_rms * norm_grad
        - tokens
        * (inv_rms * inv_rms * inv_rms)
        * jnp.mean(tokens * norm_grad, axis=-1, keepdims=True)
    )
    passed_back = passed_along(section_back.astype(jnp.bfloat16)[None], "section", -1)
    up_term = lax.dot_general(
        arrived, up_act_grad, (((0,), (0,)), ((), ())), preferred_element_type=jnp.float32
    )
    up_term = up_term.astype(jnp.bfloat16).astype(jnp.float32)
    up_grad = sum_replicas(up_term.astype(jnp.bfloat16))[None]
    return (passed_on, passed_back, up_grad)


def chip_mesh(mesh):
    sections, replicas, width = mesh.devices.shape
    return Mesh(mesh.devices.reshape(sections, replicas, width // 2, 2), ("section", "dp", "chip", "core"))


def solution(mesh):
    tokens = P("section", ("dp", "chip", "core"), None)
    return jax.shard_map(
        per_device,
        mesh=chip_mesh(mesh),
        in_specs=(
            tokens,
            P("section", None),
            tokens,
            tokens,
            P("section", None, ("chip", "core")),
            P("section", None, ("chip", "core")),
            P("section", ("chip", "core")),
            P("section", ("chip", "core"), "dp"),
            tokens,
        ),
        out_specs=(tokens, tokens, P("section", "dp", ("chip", "core"))),
        check_vma=False,
    )
```

```python
import jax
import jax.numpy as jnp
from jax import lax
from jax.sharding import Mesh, PartitionSpec as P

TSTEPS = 4


EPS = 1e-06
THETA = 0.5
SHARP = 4.0


def passed_along(value, axis, steps):
    count = lax.axis_size(axis)
    leading, last = (max(0, -steps), min(count, count - steps))
    moved = lax.ppermute(value, axis, [(source, source + steps) for source in range(leading, last)])
    receiver = lax.axis_index(axis)
    has_source = jnp.logical_and(receiver - steps >= 0, receiver - steps < count)
    return jnp.where(has_source, moved, jnp.zeros_like(moved))


def lif_rate(gate_act, up_act, leak_rate):
    drive = jax.nn.silu(gate_act) * up_act
    volts = jnp.zeros_like(drive)
    spike_sum = jnp.zeros_like(drive)
    for timestep in range(TSTEPS):
        volts = leak_rate * volts + drive
        spikes = jax.nn.sigmoid(SHARP * (volts - THETA)) - jax.nn.sigmoid(SHARP * (-volts - THETA))
        volts = volts - THETA * spikes
        spike_sum = spike_sum + spikes
    return spike_sum / TSTEPS


def swap_cores(value):
    return lax.ppermute(value, "core", [(0, 1), (1, 0)])


def shifted(value, steps):
    count = lax.axis_size("chip")
    return lax.ppermute(value, "chip", [(source, (source + steps) % count) for source in range(count)])


def to_experts(blocks):
    model_width = blocks.shape[2]
    received = [blocks[0]] + [shifted(blocks[k], k) for k in range(1, blocks.shape[0])]
    both = jnp.stack(received + [swap_cores(block) for block in received])
    return both.reshape(-1, model_width)


def combine_cores(partials, experts, capacity):
    model_width = partials.shape[1]
    paired = partials.reshape(2, experts, capacity, model_width)
    return [
        (paired[0, k] + swap_cores(paired[1, k].astype(jnp.bfloat16)).astype(jnp.float32)).astype(jnp.bfloat16)
        for k in range(experts)
    ]


def from_experts(summed):
    experts = len(summed)
    capacity, model_width = summed[0].shape
    returned = jnp.stack([summed[0]] + [shifted(summed[k], -k) for k in range(1, experts)])
    return returned.reshape(experts * capacity, model_width).astype(jnp.float32)


def dp_shifted(value, steps):
    count = lax.axis_size("dp")
    return lax.ppermute(value, "dp", [(source, (source + steps) % count) for source in range(count)])


def gather_replicas(piece):
    count = lax.axis_size("dp")
    here = lax.axis_index("dp")
    width = piece.shape[1]
    whole = jnp.zeros((piece.shape[0], width * count), piece.dtype)
    for steps in range(count):
        arrived = piece if steps == 0 else dp_shifted(piece, steps)
        whole = lax.dynamic_update_slice_in_dim(whole, arrived, ((here - steps) % count) * width, 1)
    return whole


def sum_replicas(term):
    count = lax.axis_size("dp")
    here = lax.axis_index("dp")
    rows = term.shape[0] // count
    total = lax.dynamic_slice_in_dim(term, here * rows, rows, 0).astype(jnp.float32)
    for steps in range(1, count):
        chunk = lax.dynamic_slice_in_dim(term, ((here + steps) % count) * rows, rows, 0)
        total = total + dp_shifted(chunk, steps).astype(jnp.float32)
    return total.astype(jnp.bfloat16)


def per_device(
    activations,
    norm_gain,
    route_ids,
    route_gates,
    gate_weight,
    up_weight,
    leak_rates,
    down_weight,
    cotangent,
):
    tok_count = activations.shape[1]
    model_width = activations.shape[2]
    experts = lax.axis_size("chip")
    capacity = min(tok_count, 2 * (9 * tok_count // (8 * experts)))
    tokens = activations[0].astype(jnp.float32)
    gain_row = norm_gain[0]
    inv_rms = lax.rsqrt(jnp.mean(tokens * tokens, axis=-1, keepdims=True) + EPS)
    normed = (tokens * inv_rms * gain_row).astype(jnp.bfloat16)
    flat_ids = (route_ids[0].reshape(-1) - lax.axis_index("chip")) % experts
    onehot = (flat_ids[:, None] == jnp.arange(experts, dtype=jnp.int32)[None, :]).astype(jnp.int32)
    slot_index = jnp.sum(onehot * (jnp.cumsum(onehot, axis=0) - 1), axis=1)
    places = (flat_ids * capacity + slot_index).reshape(tok_count, 2)
    positions = jnp.arange(experts * capacity, dtype=jnp.int32)[:, None]
    pick_first = positions == places[None, :, 0]
    pick_second = positions == places[None, :, 1]
    pick_both = jnp.logical_or(pick_first, pick_second)
    slot_rows = jnp.dot(
        pick_both.astype(jnp.bfloat16), normed, preferred_element_type=jnp.float32
    ).astype(jnp.bfloat16)
    arrived = to_experts(slot_rows.reshape(experts, capacity, model_width))
    gate_local = gate_weight[0]
    up_local = up_weight[0]
    leak_local = leak_rates[0]
    down_full = gather_replicas(down_weight[0])
    gate_act = jnp.dot(arrived, gate_local, preferred_element_type=jnp.float32)
    up_act = jnp.dot(arrived, up_local, preferred_element_type=jnp.float32)
    spike_rate = lif_rate(gate_act, up_act, leak_local).astype(jnp.bfloat16)
    out_part = jnp.dot(spike_rate, down_full, preferred_element_type=jnp.float32)
    out_summed = combine_cores(out_part, experts, capacity)
    weights = route_gates[0]
    upstream = cotangent[0].astype(jnp.float32)
    grad_first = (weights[:, 0:1] * upstream).astype(jnp.bfloat16)
    grad_second = (weights[:, 1:2] * upstream).astype(jnp.bfloat16)
    grad_slots = jnp.dot(
        pick_first.astype(jnp.bfloat16), grad_first, preferred_element_type=jnp.float32
    )
    grad_slots = grad_slots + jnp.dot(
        pick_second.astype(jnp.bfloat16), grad_second, preferred_element_type=jnp.float32
    )
    grad_slots, unused_arrived = lax.optimization_barrier((grad_slots.astype(jnp.bfloat16), arrived))
    grad_rows = to_experts(grad_slots.reshape(experts, capacity, model_width))
    rate_grad = lax.dot_general(
        grad_rows, down_full, (((1,), (1,)), ((), ())), preferred_element_type=jnp.float32
    )
    unused_rate, pullback = jax.vjp(
        lambda gate_in, up_in: lif_rate(gate_in, up_in, leak_local), gate_act, up_act
    )
    gate_grad, up_act_grad = pullback(rate_grad)
    gate_grad = gate_grad.astype(jnp.bfloat16)
    up_act_grad = up_act_grad.astype(jnp.bfloat16)
    back_part = lax.dot_general(
        gate_grad, gate_local, (((1,), (1,)), ((), ())), preferred_element_type=jnp.float32
    )
    back_part = back_part + lax.dot_general(
        up_act_grad, up_local, (((1,), (1,)), ((), ())), preferred_element_type=jnp.float32
    )
    out_summed, back_summed = lax.optimization_barrier(
        (out_summed, combine_cores(back_part, experts, capacity))
    )
    expert_out = from_experts(out_summed)
    back_summed, expert_out = lax.optimization_barrier((back_summed, expert_out))
    route_back = from_experts(back_summed)
    mixing = jnp.where(pick_first.T, weights[:, 0:1], 0.0) + jnp.where(
        pick_second.T, weights[:, 1:2], 0.0
    )
    moe_sum = jnp.dot(
        mixing, expert_out, precision=lax.Precision.HIGHEST, preferred_element_type=jnp.float32
    )
    section_out = (tokens + moe_sum).astype(jnp.bfloat16)
    passed_on = passed_along(section_out[None], "section", 1)
    norm_grad = (
        jnp.dot(
            pick_both.T.astype(jnp.float32),
            route_back,
            precision=lax.Precision.HIGHEST,
            preferred_element_type=jnp.float32,
        )
        * gain_row
    )
    section_back = (
        upstream
        + inv_rms * norm_grad
        - tokens
        * (inv_rms * inv_rms * inv_rms)
        * jnp.mean(tokens * norm_grad, axis=-1, keepdims=True)
    )
    passed_back = passed_along(section_back.astype(jnp.bfloat16)[None], "section", -1)
    up_term = lax.dot_general(
        arrived, up_act_grad, (((0,), (0,)), ((), ())), preferred_element_type=jnp.float32
    )
    up_term = up_term.astype(jnp.bfloat16).astype(jnp.float32)
    up_grad = sum_replicas(up_term.astype(jnp.bfloat16))[None]
    return (passed_on, passed_back, up_grad)


def chip_mesh(mesh):
    sections, replicas, width = mesh.devices.shape
    return Mesh(mesh.devices.reshape(sections, replicas, width // 2, 2), ("section", "dp", "chip", "core"))


def solution(mesh):
    tokens = P("section", ("dp", "chip", "core"), None)
    return jax.shard_map(
        per_device,
        mesh=chip_mesh(mesh),
        in_specs=(
            tokens,
            P("section", None),
            tokens,
            tokens,
            P("section", None, ("chip", "core")),
            P("section", None, ("chip", "core")),
            P("section", ("chip", "core")),
            P("section", ("chip", "core"), "dp"),
            tokens,
        ),
        out_specs=(tokens, tokens, P("section", "dp", ("chip", "core"))),
        check_vma=False,
    )
```

```python
import jax
import jax.numpy as jnp
from jax import lax
from jax.sharding import Mesh, PartitionSpec as P

TSTEPS = 4


EPS = 1e-06
THETA = 0.5
SHARP = 4.0


def passed_along(value, axis, steps):
    count = lax.axis_size(axis)
    leading, last = (max(0, -steps), min(count, count - steps))
    moved = lax.ppermute(value, axis, [(source, source + steps) for source in range(leading, last)])
    receiver = lax.axis_index(axis)
    has_source = jnp.logical_and(receiver - steps >= 0, receiver - steps < count)
    return jnp.where(has_source, moved, jnp.zeros_like(moved))


def lif_rate(gate_act, up_act, leak_rate):
    drive = jax.nn.silu(gate_act) * up_act
    volts = jnp.zeros_like(drive)
    spike_sum = jnp.zeros_like(drive)
    for timestep in range(TSTEPS):
        volts = leak_rate * volts + drive
        spikes = jax.nn.sigmoid(SHARP * (volts - THETA)) - jax.nn.sigmoid(SHARP * (-volts - THETA))
        volts = volts - THETA * spikes
        spike_sum = spike_sum + spikes
    return spike_sum / TSTEPS


def swap_cores(value):
    return lax.ppermute(value, "core", [(0, 1), (1, 0)])


def shifted(value, steps):
    count = lax.axis_size("chip")
    return lax.ppermute(value, "chip", [(source, (source + steps) % count) for source in range(count)])


def to_experts(blocks):
    model_width = blocks.shape[2]
    received = [blocks[0]] + [shifted(blocks[k], k) for k in range(1, blocks.shape[0])]
    both = jnp.stack(received + [swap_cores(block) for block in received])
    return both.reshape(-1, model_width)


def combine_cores(partials, experts, capacity):
    model_width = partials.shape[1]
    paired = partials.reshape(2, experts, capacity, model_width)
    other = swap_cores(paired[1].astype(jnp.bfloat16))
    return (paired[0] + other.astype(jnp.float32)).astype(jnp.bfloat16)


def from_experts(summed):
    experts, capacity, model_width = summed.shape
    returned = jnp.stack([summed[0]] + [shifted(summed[k], -k) for k in range(1, experts)])
    return returned.reshape(experts * capacity, model_width).astype(jnp.float32)


def dp_shifted(value, steps):
    count = lax.axis_size("dp")
    return lax.ppermute(value, "dp", [(source, (source + steps) % count) for source in range(count)])


def gather_replicas(piece):
    count = lax.axis_size("dp")
    here = lax.axis_index("dp")
    width = piece.shape[1]
    whole = jnp.zeros((piece.shape[0], width * count), piece.dtype)
    for steps in range(count):
        arrived = piece if steps == 0 else dp_shifted(piece, steps)
        whole = lax.dynamic_update_slice_in_dim(whole, arrived, ((here - steps) % count) * width, 1)
    return whole


def sum_replicas(term):
    count = lax.axis_size("dp")
    here = lax.axis_index("dp")
    rows = term.shape[0] // count
    total = lax.dynamic_slice_in_dim(term, here * rows, rows, 0).astype(jnp.float32)
    for steps in range(1, count):
        chunk = lax.dynamic_slice_in_dim(term, ((here + steps) % count) * rows, rows, 0)
        total = total + dp_shifted(chunk, steps).astype(jnp.float32)
    return total.astype(jnp.bfloat16)


def per_device(
    activations,
    norm_gain,
    route_ids,
    route_gates,
    gate_weight,
    up_weight,
    leak_rates,
    down_weight,
    cotangent,
):
    tok_count = activations.shape[1]
    model_width = activations.shape[2]
    experts = lax.axis_size("chip")
    capacity = min(tok_count, 2 * (9 * tok_count // (8 * experts)))
    tokens = activations[0].astype(jnp.float32)
    gain_row = norm_gain[0]
    inv_rms = lax.rsqrt(jnp.mean(tokens * tokens, axis=-1, keepdims=True) + EPS)
    normed = (tokens * inv_rms * gain_row).astype(jnp.bfloat16)
    flat_ids = (route_ids[0].reshape(-1) - lax.axis_index("chip")) % experts
    onehot = (flat_ids[:, None] == jnp.arange(experts, dtype=jnp.int32)[None, :]).astype(jnp.int32)
    slot_index = jnp.sum(onehot * (jnp.cumsum(onehot, axis=0) - 1), axis=1)
    places = (flat_ids * capacity + slot_index).reshape(tok_count, 2)
    positions = jnp.arange(experts * capacity, dtype=jnp.int32)[:, None]
    pick_first = positions == places[None, :, 0]
    pick_second = positions == places[None, :, 1]
    pick_both = jnp.logical_or(pick_first, pick_second)
    slot_rows = jnp.dot(
        pick_both.astype(jnp.bfloat16), normed, preferred_element_type=jnp.float32
    ).astype(jnp.bfloat16)
    arrived = to_experts(slot_rows.reshape(experts, capacity, model_width))
    gate_local = gate_weight[0]
    up_local = up_weight[0]
    leak_local = leak_rates[0]
    down_full = gather_replicas(down_weight[0])
    gate_act = jnp.dot(arrived, gate_local, preferred_element_type=jnp.float32)
    up_act = jnp.dot(arrived, up_local, preferred_element_type=jnp.float32)
    spike_exact, lif_pullback = jax.vjp(
        lambda gate_in, up_in: lif_rate(gate_in, up_in, leak_local), gate_act, up_act
    )
    spike_rate = spike_exact.astype(jnp.bfloat16)
    gate_slope, up_slope = lif_pullback(jnp.ones_like(spike_exact))
    out_part = jnp.dot(spike_rate, down_full, preferred_element_type=jnp.float32)
    out_summed = combine_cores(out_part, experts, capacity)
    weights = route_gates[0]
    upstream = cotangent[0].astype(jnp.float32)
    grad_first = (weights[:, 0:1] * upstream).astype(jnp.bfloat16)
    grad_second = (weights[:, 1:2] * upstream).astype(jnp.bfloat16)
    grad_slots = jnp.dot(
        pick_first.astype(jnp.bfloat16), grad_first, preferred_element_type=jnp.float32
    )
    grad_slots = grad_slots + jnp.dot(
        pick_second.astype(jnp.bfloat16), grad_second, preferred_element_type=jnp.float32
    )
    grad_slots, unused_arrived = lax.optimization_barrier((grad_slots.astype(jnp.bfloat16), arrived))
    grad_rows = to_experts(grad_slots.reshape(experts, capacity, model_width))
    rate_grad = lax.dot_general(
        grad_rows, down_full, (((1,), (1,)), ((), ())), preferred_element_type=jnp.float32
    )
    gate_grad = (rate_grad * gate_slope).astype(jnp.bfloat16)
    up_act_grad = (rate_grad * up_slope).astype(jnp.bfloat16)
    back_part = lax.dot_general(
        gate_grad, gate_local, (((1,), (1,)), ((), ())), preferred_element_type=jnp.float32
    )
    back_part = back_part + lax.dot_general(
        up_act_grad, up_local, (((1,), (1,)), ((), ())), preferred_element_type=jnp.float32
    )
    out_summed, back_summed = lax.optimization_barrier(
        (out_summed, combine_cores(back_part, experts, capacity))
    )
    expert_out = from_experts(out_summed)
    back_summed, expert_out = lax.optimization_barrier((back_summed, expert_out))
    route_back = from_experts(back_summed)
    mixing = jnp.where(pick_first.T, weights[:, 0:1], 0.0) + jnp.where(
        pick_second.T, weights[:, 1:2], 0.0
    )
    moe_sum = jnp.dot(
        mixing, expert_out, precision=lax.Precision.HIGHEST, preferred_element_type=jnp.float32
    )
    section_out = (tokens + moe_sum).astype(jnp.bfloat16)
    passed_on = passed_along(section_out[None], "section", 1)
    norm_grad = (
        jnp.dot(
            pick_both.T.astype(jnp.float32),
            route_back,
            precision=lax.Precision.HIGHEST,
            preferred_element_type=jnp.float32,
        )
        * gain_row
    )
    section_back = (
        upstream
        + inv_rms * norm_grad
        - tokens
        * (inv_rms * inv_rms * inv_rms)
        * jnp.mean(tokens * norm_grad, axis=-1, keepdims=True)
    )
    passed_back = passed_along(section_back.astype(jnp.bfloat16)[None], "section", -1)
    up_term = lax.dot_general(
        arrived, up_act_grad, (((0,), (0,)), ((), ())), preferred_element_type=jnp.float32
    )
    up_term = up_term.astype(jnp.bfloat16).astype(jnp.float32)
    up_grad = sum_replicas(up_term.astype(jnp.bfloat16))[None]
    return (passed_on, passed_back, up_grad)


def chip_mesh(mesh):
    sections, replicas, width = mesh.devices.shape
    return Mesh(mesh.devices.reshape(sections, replicas, width // 2, 2), ("section", "dp", "chip", "core"))


def solution(mesh):
    tokens = P("section", ("dp", "chip", "core"), None)
    return jax.shard_map(
        per_device,
        mesh=chip_mesh(mesh),
        in_specs=(
            tokens,
            P("section", None),
            tokens,
            tokens,
            P("section", None, ("chip", "core")),
            P("section", None, ("chip", "core")),
            P("section", ("chip", "core")),
            P("section", ("chip", "core"), "dp"),
            tokens,
        ),
        out_specs=(tokens, tokens, P("section", "dp", ("chip", "core"))),
        check_vma=False,
    )
```
